32 devices in a mesh: search: 4 (over y, core), net: 8 (over z, x).
Axes of the slice: x: 2, y: 2, z: 4, core: 2. Of those that a mesh axis runs over, the one named last changes fastest.
Arguments:
- states: bfloat16 [4096, 11552], P(('search', 'net')), may hold values from -6 to 6
- counts: int32 [32], P(('search', 'net')), may hold values from 1 to 128, 1024 in all
- owners: int32 [4096], P(('search', 'net')), may hold values from 0 to 255
- legal: int32 [4096, 8, 361], P(('search', 'net')), may hold values 0 or 1
- in_weight: bfloat16 [3, 3, 32, 256], replicated, may hold values from -0.375 to 0.375
- mid_weight: bfloat16 [1, 3, 3, 256, 256], replicated, may hold values from -0.125 to 0.125
- out_weight: bfloat16 [1, 3, 3, 256, 256], replicated, may hold values from -0.125 to 0.125
- policy_weight: bfloat16 [256, 8], replicated, may hold values from -0.75 to 0.75
- pass_weight: bfloat16 [256, 8], replicated, may hold values from -1.5 to 1.5
- value_weight: bfloat16 [256], replicated, may hold values from -1.5 to 1.5
- logit_scale: float32 [8], replicated, may hold values from 0.25 to 4
Outputs:
- priors: float32 [4096, 8, 362], P(('search', 'net'))
- leaf_values: float32 [4096], P(('search', 'net'))
- tree_value: float32 [256], P(('search', 'net'))
The draws below stay inside these ranges and needn't reach their ends.
Inputs may be any that keep to these rules, and one draw needn't show every extreme that they name: counts sum to exactly 32 times the number of devices, and one device holds 128 live leaves.
All inputs are finite; a program needn't handle non-finite values. No bound on the sum of `legal` on one device may be relied on, other than what follows from the above.
Results may differ from the reference program's by a relative error of at most 0.03.
Values may be sent and summed in bfloat16 or wider, within the bound.
No kernel may reach another device: no remote copies, remote signals or barrier semaphores. Data moves between devices by JAX's collectives and lax.ppermute only.
A program may use at most 128 MiB of HBM per device.

```python
import math
import jax
import jax.numpy as jnp
import numpy as np
from jax import lax

SIDE = 19
BOARD = 361
MOVES = 362
PLANES = 32
CH = 256
FACT = 8
BLOCKS = 1
LIVE_DEV = 32
SLOT_DEV = 128
SLOTS = 4096
TREES = 256
DEVICES = 32


def set_ends(entries, rng, smallest, high):
    place = [jax.random.randint(jax.random.fold_in(rng, axis), (), 0, length) for axis, length in enumerate(entries.shape)]
    widest = entries.shape.index(max(entries.shape))
    neighbour = place[:widest] + [(place[widest] + 1) % entries.shape[widest]] + place[widest + 1:]
    return entries.at[tuple(place)].set(smallest).at[tuple(neighbour)].set(high)


def levels(stream_key, dims, split, least, largest):
    def one(axis_at, blocks):
        draws = jax.random.uniform(jax.random.fold_in(jax.random.fold_in(stream_key, 6), axis_at), (blocks,), jnp.float32, least / len(split), largest / len(split))
        return jnp.repeat(jnp.exp(draws), dims[axis_at] // blocks).reshape((-1,) + (1,) * (len(dims) - axis_at - 1))

    level = one(*split[0])
    for cut in split[1:]:
        level = level * one(*cut)
    return level


def profile(number_of, total, limit, lean):
    weights = [(1 << 20) // math.isqrt(standing ** lean) + 1 for standing in range(2, number_of + 1)]
    surplus, given = total - limit - (number_of - 1), [1] * (number_of - 1)
    while surplus > 0:
        movable = [i for i in range(number_of - 1) if given[i] < limit]
        whole, left = sum([weights[i] for i in movable]), surplus
        for i in movable:
            more = min(limit - given[i], max(1, left * weights[i] // whole), surplus)
            given[i] = given[i] + more
            surplus = surplus - more
    return np.array([limit] + given)


def uneven(rng, amount, total, limit, lean):
    if amount == 2:
        one = jax.random.randint(rng, (), max(1, total - limit), min(limit, total - 1) + 1)
        return jnp.stack([one, total - one])
    sizes = jnp.asarray(profile(amount, total, limit, lean), jnp.int32)
    couples = (amount - 1) // 2
    donor, sink = sizes[1:1 + 2 * couples:2], sizes[2:2 + 2 * couples:2]
    margin = jnp.minimum(donor - 1, limit - sink)
    shifted = jax.random.randint(jax.random.fold_in(rng, 1), (couples,), 0, 1 << 20) % (margin + 1)
    sizes = sizes.at[1:1 + 2 * couples:2].set(donor - shifted).at[2:2 + 2 * couples:2].set(sink + shifted)
    return sizes[jax.random.permutation(jax.random.fold_in(rng, 2), amount)]


def normal_values(own_key, shape, scale, reach, cuts=(), kind=jnp.bfloat16):
    entries = jax.random.normal(own_key, shape, jnp.float32) * scale
    if len(cuts) > 0:
        entries = levels(own_key, shape, cuts, -0.22, 0.18) * entries
    return jnp.clip(entries, min=-reach, max=reach).astype(kind)


def setup_inputs(seed: int = 0) -> dict:
    arg_keys = jax.random.split(jax.random.key(seed), 12)
    states = normal_values(arg_keys[0], (SLOTS, BOARD * PLANES), 1.0, 6.0, ((0, 32),))
    counts = uneven(arg_keys[1], DEVICES, LIVE_DEV * DEVICES, SLOT_DEV, 2).astype(jnp.int32)
    owners = set_ends(jax.random.randint(arg_keys[2], (SLOTS,), 0, TREES), jax.random.fold_in(arg_keys[2], 1), 0, TREES - 1).astype(jnp.int32)
    legal = set_ends((jax.random.randint(arg_keys[3], (SLOTS, FACT, BOARD), 0, 2) < 1).astype(jnp.int32), jax.random.fold_in(arg_keys[3], 1), 0, 1)
    in_weight = normal_values(arg_keys[4], (SIDE // 6, SIDE // 6, PLANES, CH), (9 * PLANES) ** -0.5, 0.375)
    mid_weight = normal_values(arg_keys[5], (BLOCKS, SIDE // 6, SIDE // 6, CH, CH), (9 * CH) ** -0.5, 0.125)
    out_weight = normal_values(arg_keys[6], (BLOCKS, SIDE // 6, SIDE // 6, CH, CH), (9 * CH) ** -0.5, 0.125)
    policy_weight = normal_values(arg_keys[7], (CH, FACT), (CH // 4) ** -0.5, 0.75)
    pass_weight = normal_values(arg_keys[8], (CH, FACT), (CH // 16) ** -0.5, 1.5)
    value_weight = normal_values(arg_keys[9], (CH,), (CH // 16) ** -0.5, 1.5)
    logit_scale = jnp.clip(jnp.exp(jax.random.uniform(arg_keys[10], (FACT,), jnp.float32, math.log(0.25), math.log(4.0))), 0.25, 4.0)
    return dict(states=states, counts=counts, owners=owners, legal=legal, in_weight=in_weight, mid_weight=mid_weight, out_weight=out_weight, policy_weight=policy_weight, pass_weight=pass_weight, value_weight=value_weight, logit_scale=logit_scale)


def convolve(inputs, kernel):
    return lax.conv_general_dilated(inputs, kernel, (1, 1), "SAME", dimension_numbers=("NHWC", "HWIO", "NHWC"), preferred_element_type=jnp.float32)


def evaluate(batch, in_weight, mid_weight, out_weight, policy_weight, pass_weight, value_weight):
    leaves = batch.shape[0]
    board = batch.reshape(leaves, SIDE, SIDE, PLANES)
    hidden = jax.nn.relu(convolve(board, in_weight)).astype(jnp.bfloat16)
    for block in range(BLOCKS):
        inner = jax.nn.relu(convolve(hidden, mid_weight[block])).astype(jnp.bfloat16)
        hidden = jax.nn.relu(hidden.astype(jnp.float32) + convolve(inner, out_weight[block])).astype(jnp.bfloat16)
    cells = jnp.einsum("bhwc,cf->bfhw", hidden.astype(jnp.float32), policy_weight.astype(jnp.float32), precision=lax.Precision.HIGHEST).reshape(leaves, FACT, BOARD)
    pooled = jnp.mean(hidden, axis=(1, 2), dtype=jnp.float32)
    passing = jnp.dot(pooled, pass_weight.astype(jnp.float32), precision=lax.Precision.HIGHEST)
    logits = jnp.concatenate([cells, passing[:, :, None]], axis=2).astype(jnp.bfloat16)
    values = jnp.tanh(jnp.dot(pooled, value_weight.astype(jnp.float32), precision=lax.Precision.HIGHEST)).astype(jnp.bfloat16)
    return logits, values


def masked_priors(logits, legal, logit_scale):
    scaled = logit_scale[None, :, None] * logits.astype(jnp.float32)
    allowed = jnp.concatenate([legal > 0, jnp.ones(legal.shape[:2] + (1,), dtype=jnp.bool_)], axis=2)
    peak = jnp.max(jnp.where(allowed, scaled, -1e30), axis=2, keepdims=True)
    weights = jnp.exp(jnp.where(allowed, scaled - peak, -1e30))
    return weights / jnp.sum(weights, axis=2, keepdims=True)


def reference(states, counts, owners, legal, in_weight, mid_weight, out_weight, policy_weight, pass_weight, value_weight, logit_scale):
    total = LIVE_DEV * DEVICES
    finish = jnp.cumsum(counts).astype(jnp.int32)
    begin = (finish - counts).astype(jnp.int32)
    ranks = jnp.arange(total, dtype=jnp.int32)
    source = jnp.sum((finish[None, :] <= ranks[:, None]).astype(jnp.int32), axis=1).astype(jnp.int32)
    picked = (source * SLOT_DEV + ranks - begin[source]).astype(jnp.int32)
    compact = states[picked].reshape(DEVICES, LIVE_DEV, BOARD * PLANES)

    def run_batch(batch):
        return evaluate(batch, in_weight, mid_weight, out_weight, policy_weight, pass_weight, value_weight)

    logits, values = lax.map(run_batch, compact)
    logits = logits.reshape(total, FACT, MOVES)
    values = values.reshape(total)
    slot_ids = jnp.arange(SLOTS, dtype=jnp.int32)
    device_of = slot_ids // SLOT_DEV
    within = slot_ids % SLOT_DEV
    alive = within < counts[device_of]
    rank_of = jnp.minimum(begin[device_of] + within, total - 1).astype(jnp.int32)
    priors = masked_priors(logits[rank_of], legal, logit_scale) * alive[:, None, None].astype(jnp.float32)
    leaf_values = jnp.where(alive, values[rank_of].astype(jnp.float32), 0.0)
    tree_value = jax.ops.segment_sum(leaf_values, owners, TREES)
    return priors, leaf_values, tree_value
```

```python
import jax
import jax.numpy as jnp
from jax import lax
from jax.sharding import PartitionSpec as P

SIDE = 19
BOARD = 361
PLANES = 32
FACT = 8
TREE_DEV = 8


def convolve(inputs, kernel):
    return lax.conv_general_dilated(
        inputs,
        kernel,
        (1, 1),
        "SAME",
        dimension_numbers=("NHWC", "HWIO", "NHWC"),
        preferred_element_type=jnp.float32,
    )


def evaluate(batch, in_weight, mid_weight, out_weight, policy_weight, pass_weight, value_weight):
    leaves = batch.shape[0]
    board = batch.reshape(leaves, SIDE, SIDE, PLANES)
    hidden = jax.nn.relu(convolve(board, in_weight)).astype(jnp.bfloat16)
    inner = jax.nn.relu(convolve(hidden, mid_weight[0])).astype(jnp.bfloat16)
    hidden = jax.nn.relu(hidden.astype(jnp.float32) + convolve(inner, out_weight[0])).astype(
        jnp.bfloat16
    )
    cells = jnp.einsum(
        "bhwc,cf->bfhw", hidden, policy_weight, preferred_element_type=jnp.float32
    ).reshape(leaves, FACT, BOARD)
    pooled = jnp.mean(hidden, axis=(1, 2), dtype=jnp.float32)
    passing = jnp.dot(pooled, pass_weight.astype(jnp.float32), precision=lax.Precision.HIGHEST)
    logits = jnp.concatenate([cells, passing[:, :, None]], axis=2).astype(jnp.bfloat16)
    values = jnp.tanh(
        jnp.dot(pooled, value_weight.astype(jnp.float32), precision=lax.Precision.HIGHEST)
    ).astype(jnp.bfloat16)
    return (logits, values)


def masked_priors(logits, legal, logit_scale):
    scaled = logit_scale[None, :, None] * logits.astype(jnp.float32)
    allowed = jnp.concatenate(
        [legal > 0, jnp.ones(legal.shape[:2] + (1,), dtype=jnp.bool_)], axis=2
    )
    peak = jnp.max(jnp.where(allowed, scaled, -1e30), axis=2, keepdims=True)
    weights = jnp.exp(jnp.where(allowed, scaled - peak, -1e30))
    return weights / jnp.sum(weights, axis=2, keepdims=True)


def body(
    states,
    counts,
    owners,
    legal,
    in_weight,
    mid_weight,
    out_weight,
    policy_weight,
    pass_weight,
    value_weight,
    logit_scale,
):
    slot_count = states.shape[0]
    own_count = counts[0]
    slot_index = jnp.arange(slot_count, dtype=jnp.int32)
    returned_logits, returned_values = evaluate(
        states, in_weight, mid_weight, out_weight, policy_weight, pass_weight, value_weight
    )
    alive = slot_index < own_count
    priors = masked_priors(returned_logits, legal, logit_scale) * alive[:, None, None].astype(
        jnp.float32
    )
    leaf_values = jnp.where(alive, returned_values.astype(jnp.float32), 0.0)
    tree_total = TREE_DEV * lax.axis_size(("search", "net"))
    onehot = (owners[:, None] == jnp.arange(tree_total, dtype=jnp.int32)[None, :]).astype(
        jnp.float32
    )
    partial_sums = jnp.dot(leaf_values, onehot, precision=lax.Precision.HIGHEST)
    groups = lax.axis_size(("search", "net"))
    spread = lax.all_to_all(
        partial_sums.reshape(groups, TREE_DEV), ("search", "net"), 0, 0, tiled=True
    )
    tree_value = jnp.sum(spread, axis=0)
    return (priors, leaf_values, tree_value)


def solution(mesh):
    in_specs = (
        P(("search", "net"), None),
        P(("search", "net")),
        P(("search", "net")),
        P(("search", "net"), None, None),
        P(),
        P(),
        P(),
        P(),
        P(),
        P(),
        P(),
    )
    out_specs = (P(("search", "net"), None, None), P(("search", "net")), P(("search", "net")))
    return jax.shard_map(body, mesh=mesh, in_specs=in_specs, out_specs=out_specs, check_vma=False)
```

```python
import functools

import jax
import jax.numpy as jnp
from jax import lax
from jax.experimental import pallas as pl
from jax.experimental.pallas import tpu as pltpu
from jax.sharding import PartitionSpec as P

SIDE = 19
BOARD = 361
MOVES = 362
PLANES = 32
FACT = 8
TREE_DEV = 8
AXES = ("search", "net")
CHUNK = 8
PASSES = 3
CORE_CAP = 64
LINK_CAP = 24


def convolve(inputs, kernel):
    return lax.conv_general_dilated(
        inputs,
        kernel,
        (1, 1),
        "SAME",
        dimension_numbers=("NHWC", "HWIO", "NHWC"),
        preferred_element_type=jnp.float32,
    )


def evaluate(batch, in_weight, mid_weight, out_weight, policy_weight, pass_weight, value_weight):
    leaves = batch.shape[0]
    board = batch.reshape(leaves, SIDE, SIDE, PLANES)
    hidden = jax.nn.relu(convolve(board, in_weight)).astype(jnp.bfloat16)
    inner = jax.nn.relu(convolve(hidden, mid_weight[0])).astype(jnp.bfloat16)
    hidden = jax.nn.relu(hidden.astype(jnp.float32) + convolve(inner, out_weight[0])).astype(
        jnp.bfloat16
    )
    cells = jnp.einsum(
        "bhwc,cf->bfhw", hidden, policy_weight, preferred_element_type=jnp.float32
    ).reshape(leaves, FACT, BOARD)
    pooled = jnp.mean(hidden, axis=(1, 2), dtype=jnp.float32)
    passing = jnp.dot(pooled, pass_weight.astype(jnp.float32), precision=lax.Precision.HIGHEST)
    logits = jnp.concatenate([cells, passing[:, :, None]], axis=2).astype(jnp.bfloat16)
    values = jnp.tanh(
        jnp.dot(pooled, value_weight.astype(jnp.float32), precision=lax.Precision.HIGHEST)
    ).astype(jnp.bfloat16)
    return (logits, values)


def masked_priors(logits, legal, logit_scale):
    scaled = logit_scale[None, :, None] * logits.astype(jnp.float32)
    allowed = jnp.concatenate(
        [legal > 0, jnp.ones(legal.shape[:2] + (1,), dtype=jnp.bool_)], axis=2
    )
    peak = jnp.max(jnp.where(allowed, scaled, -1e30), axis=2, keepdims=True)
    weights = jnp.exp(jnp.where(allowed, scaled - peak, -1e30))
    return weights / jnp.sum(weights, axis=2, keepdims=True)


def plan_kernel(masks, caps, counts_ref, out_ref):
    counts_all = counts_ref[...]
    lanes = counts_all.shape[1]
    lane = lax.broadcasted_iota(jnp.int32, counts_all.shape, 1)

    def swap(x, mask):
        up = pltpu.roll(x, mask, 1)
        up_from = pltpu.roll(lane, mask, 1)
        down = pltpu.roll(x, lanes - mask, 1)
        return jnp.where(up_from == (lane ^ mask), up, down)

    flows = [jnp.zeros_like(counts_all) for _ in masks]
    for _ in range(PASSES):
        for e, (mask, cap) in enumerate(zip(masks, caps)):
            sent = sum(flows)
            got = sum(swap(f, m) for f, m in zip(flows, masks))
            load = counts_all - sent + got
            own = counts_all - sent
            move = jnp.right_shift(jnp.maximum(load - swap(load, mask), 0), 1)
            cancel = jnp.minimum(move, swap(flows[e], mask))
            add = jnp.clip(move - cancel, 0, jnp.minimum(cap - flows[e], own))
            flows[e] = flows[e] + add - swap(cancel, mask)
    rows = flows + [swap(f, m) for f, m in zip(flows, masks)]
    rows = rows + [jnp.zeros_like(counts_all)] * (out_ref.shape[0] - len(rows))
    out_ref[...] = jnp.concatenate(rows, axis=0)


def make_plan(counts_all, masks, caps):
    groups = counts_all.shape[0]
    lanes = -(-groups // 128) * 128
    padded = jnp.zeros((1, lanes), jnp.int32).at[0, :groups].set(counts_all)
    rows = -(-2 * len(masks) // 8) * 8
    return pl.pallas_call(
        functools.partial(plan_kernel, masks, caps),
        out_shape=jax.ShapeDtypeStruct((rows, lanes), jnp.int32),
    )(padded)


def body(
    states,
    counts,
    owners,
    legal,
    in_weight,
    mid_weight,
    out_weight,
    policy_weight,
    pass_weight,
    value_weight,
    logit_scale,
):
    weights = (in_weight, mid_weight, out_weight, policy_weight, pass_weight, value_weight)
    slot_count, row = states.shape
    groups = lax.axis_size(AXES)
    net_size = lax.axis_size("net")
    me = lax.axis_index(AXES)
    own_count = counts[0]

    counts_all = lax.all_to_all(
        jnp.broadcast_to(counts, (groups, 1)), AXES, 0, 0, tiled=True
    ).reshape(groups)

    masks = (4, 2, 2 * net_size, 1, net_size)
    caps = (LINK_CAP, LINK_CAP, LINK_CAP, LINK_CAP, CORE_CAP)
    plan = make_plan(counts_all, masks, caps)
    mine = lax.dynamic_slice(plan, (0, me), (plan.shape[0], 1))
    send = [mine[e, 0] for e in range(len(masks))]
    recv = [mine[len(masks) + e, 0] for e in range(len(masks))]
    keep = own_count - sum(send)

    starts = []
    offset = keep
    for e in range(len(masks)):
        starts.append(offset)
        offset = offset + send[e]
    pairs = [[(d, d ^ m) for d in range(groups)] for m in masks]
    incoming = []
    for e, cap in enumerate(caps):
        idx = jnp.clip(starts[e] + jnp.arange(cap, dtype=jnp.int32), 0, slot_count - 1)
        outgoing = jnp.take(states, idx, axis=0)
        incoming.append(lax.ppermute(outgoing, AXES, pairs[e]))

    full = keep // CHUNK
    rem = keep - full * CHUNK

    def own_step(t, carry):
        logits_acc, values_acc = carry
        rows = lax.dynamic_slice(states, (t * CHUNK, 0), (CHUNK, row))
        logits, values = evaluate(rows, *weights)
        logits_acc = lax.dynamic_update_slice(logits_acc, logits, (t * CHUNK, 0, 0))
        values_acc = lax.dynamic_update_slice(values_acc, values, (t * CHUNK,))
        return logits_acc, values_acc

    own_logits, own_values = lax.fori_loop(
        0,
        full,
        own_step,
        (
            jnp.zeros((slot_count, FACT, MOVES), jnp.bfloat16),
            jnp.zeros((slot_count,), jnp.bfloat16),
        ),
    )

    tail_idx = jnp.clip(full * CHUNK + jnp.arange(CHUNK, dtype=jnp.int32), 0, slot_count - 1)
    pool = jnp.concatenate([jnp.take(states, tail_idx, axis=0)] + incoming, axis=0)
    pool_rows = pool.shape[0]
    work_rows = -(-pool_rows // CHUNK) * CHUNK
    k = jnp.arange(work_rows, dtype=jnp.int32)
    work_idx = jnp.where(k < rem, k, 0)
    seg_start = rem
    base = CHUNK
    recv_pos = []
    for e, cap in enumerate(caps):
        inside = (k >= seg_start) & (k < seg_start + recv[e])
        work_idx = jnp.where(inside, base + k - seg_start, work_idx)
        recv_pos.append(seg_start)
        seg_start = seg_start + recv[e]
        base = base + cap
    work_count = seg_start
    work_idx = jnp.clip(work_idx, 0, pool_rows - 1)

    def work_step(t, carry):
        logits_acc, values_acc = carry
        idx = lax.dynamic_slice(work_idx, (t * CHUNK,), (CHUNK,))
        rows = jnp.take(pool, idx, axis=0)
        logits, values = evaluate(rows, *weights)
        logits_acc = lax.dynamic_update_slice(logits_acc, logits, (t * CHUNK, 0, 0))
        values_acc = lax.dynamic_update_slice(values_acc, values, (t * CHUNK,))
        return logits_acc, values_acc

    work_logits, work_values = lax.fori_loop(
        0,
        (work_count + CHUNK - 1) // CHUNK,
        work_step,
        (
            jnp.zeros((work_rows, FACT, MOVES), jnp.bfloat16),
            jnp.zeros((work_rows,), jnp.bfloat16),
        ),
    )

    back_logits = []
    back_values = []
    for e, cap in enumerate(caps):
        idx = jnp.clip(recv_pos[e] + jnp.arange(cap, dtype=jnp.int32), 0, work_rows - 1)
        back_logits.append(lax.ppermute(jnp.take(work_logits, idx, axis=0), AXES, pairs[e]))
        back_values.append(lax.ppermute(jnp.take(work_values, idx, axis=0), AXES, pairs[e]))

    all_logits = jnp.concatenate([own_logits, work_logits] + back_logits, axis=0)
    all_values = jnp.concatenate([own_values, work_values] + back_values, axis=0)
    slot = jnp.arange(slot_count, dtype=jnp.int32)
    pick = jnp.where(slot < full * CHUNK, slot, slot_count + slot - full * CHUNK)
    base = slot_count + work_rows
    for e, cap in enumerate(caps):
        inside = (slot >= starts[e]) & (slot < starts[e] + send[e])
        pick = jnp.where(inside, base + slot - starts[e], pick)
        base = base + cap
    pick = jnp.clip(pick, 0, all_logits.shape[0] - 1)
    slot_logits = jnp.take(all_logits, pick, axis=0)
    slot_values = jnp.take(all_values, pick, axis=0)

    alive = slot < own_count
    priors = jnp.where(
        alive[:, None, None], masked_priors(slot_logits, legal, logit_scale), 0.0
    )
    leaf_values = jnp.where(alive, slot_values.astype(jnp.float32), 0.0)
    tree_total = TREE_DEV * groups
    onehot = (owners[:, None] == jnp.arange(tree_total, dtype=jnp.int32)[None, :]).astype(
        jnp.float32
    )
    partial_sums = jnp.dot(leaf_values, onehot, precision=lax.Precision.HIGHEST)
    spread = lax.all_to_all(partial_sums.reshape(groups, TREE_DEV), AXES, 0, 0, tiled=True)
    tree_value = jnp.sum(spread, axis=0)
    return (priors, leaf_values, tree_value)


def solution(mesh):
    in_specs = (
        P(AXES, None),
        P(AXES),
        P(AXES),
        P(AXES, None, None),
        P(),
        P(),
        P(),
        P(),
        P(),
        P(),
        P(),
    )
    out_specs = (P(AXES, None, None), P(AXES), P(AXES))
    return jax.shard_map(body, mesh=mesh, in_specs=in_specs, out_specs=out_specs, check_vma=False)
```

```python
import functools

import jax
import jax.numpy as jnp
from jax import lax
from jax.experimental import pallas as pl
from jax.experimental.pallas import tpu as pltpu
from jax.sharding import PartitionSpec as P

SIDE = 19
BOARD = 361
MOVES = 362
PLANES = 32
FACT = 8
TREE_DEV = 8
AXES = ("search", "net")
CHUNK = 40
PASSES = 3
CORE_CAP = 64
LINK_CAP = 28


def convolve(inputs, kernel):
    return lax.conv_general_dilated(
        inputs,
        kernel,
        (1, 1),
        "SAME",
        dimension_numbers=("NHWC", "HWIO", "NHWC"),
        preferred_element_type=jnp.float32,
    )


def evaluate(batch, in_weight, mid_weight, out_weight, policy_weight, pass_weight, value_weight):
    leaves = batch.shape[0]
    board = batch.reshape(leaves, SIDE, SIDE, PLANES)
    hidden = jax.nn.relu(convolve(board, in_weight)).astype(jnp.bfloat16)
    inner = jax.nn.relu(convolve(hidden, mid_weight[0])).astype(jnp.bfloat16)
    hidden = jax.nn.relu(hidden.astype(jnp.float32) + convolve(inner, out_weight[0])).astype(
        jnp.bfloat16
    )
    cells = jnp.einsum(
        "bhwc,cf->bfhw", hidden, policy_weight, preferred_element_type=jnp.float32
    ).reshape(leaves, FACT, BOARD)
    pooled = jnp.mean(hidden, axis=(1, 2), dtype=jnp.float32)
    passing = jnp.dot(pooled, pass_weight.astype(jnp.float32), precision=lax.Precision.HIGHEST)
    logits = jnp.concatenate([cells, passing[:, :, None]], axis=2).astype(jnp.bfloat16)
    values = jnp.tanh(
        jnp.dot(pooled, value_weight.astype(jnp.float32), precision=lax.Precision.HIGHEST)
    ).astype(jnp.bfloat16)
    return (logits, values)


def masked_priors(logits, legal, logit_scale):
    scaled = logit_scale[None, :, None] * logits.astype(jnp.float32)
    allowed = jnp.concatenate(
        [legal > 0, jnp.ones(legal.shape[:2] + (1,), dtype=jnp.bool_)], axis=2
    )
    peak = jnp.max(jnp.where(allowed, scaled, -1e30), axis=2, keepdims=True)
    weights = jnp.exp(jnp.where(allowed, scaled - peak, -1e30))
    return weights / jnp.sum(weights, axis=2, keepdims=True)


def plan_kernel(masks, caps, counts_ref, out_ref):
    counts_all = counts_ref[...]
    lanes = counts_all.shape[1]
    lane = lax.broadcasted_iota(jnp.int32, counts_all.shape, 1)

    def swap(x, mask):
        up = pltpu.roll(x, mask, 1)
        up_from = pltpu.roll(lane, mask, 1)
        down = pltpu.roll(x, lanes - mask, 1)
        return jnp.where(up_from == (lane ^ mask), up, down)

    flows = [jnp.zeros_like(counts_all) for _ in masks]
    for _ in range(PASSES):
        for e, (mask, cap) in enumerate(zip(masks, caps)):
            sent = sum(flows)
            got = sum(swap(f, m) for f, m in zip(flows, masks))
            load = counts_all - sent + got
            own = counts_all - sent
            move = jnp.right_shift(jnp.maximum(load - swap(load, mask), 0), 1)
            cancel = jnp.minimum(move, swap(flows[e], mask))
            add = jnp.clip(move - cancel, 0, jnp.minimum(cap - flows[e], own))
            flows[e] = flows[e] + add - swap(cancel, mask)
    into = [swap(f, m) for f, m in zip(flows, masks)]
    keep = counts_all - sum(flows)
    starts, places = [], []
    for e in range(len(masks)):
        starts.append(keep + sum(flows[:e]))
        places.append(keep + sum(into[:e]))
    rows = flows + into + starts + places + [keep, keep + sum(into)]
    rows = rows + [jnp.zeros_like(counts_all)] * (out_ref.shape[0] - len(rows))
    out_ref[...] = jnp.concatenate(rows, axis=0)


def make_plan(counts_all, masks, caps):
    groups = counts_all.shape[0]
    lanes = -(-groups // 128) * 128
    padded = jnp.zeros((1, lanes), jnp.int32).at[0, :groups].set(counts_all)
    rows = -(-(4 * len(masks) + 2) // 8) * 8
    return pl.pallas_call(
        functools.partial(plan_kernel, masks, caps),
        out_shape=jax.ShapeDtypeStruct((rows, lanes), jnp.int32),
    )(padded)


def body(
    states,
    counts,
    owners,
    legal,
    in_weight,
    mid_weight,
    out_weight,
    policy_weight,
    pass_weight,
    value_weight,
    logit_scale,
):
    weights = (in_weight, mid_weight, out_weight, policy_weight, pass_weight, value_weight)
    slot_count, row = states.shape
    groups = lax.axis_size(AXES)
    net_size = lax.axis_size("net")
    me = lax.axis_index(AXES)
    own_count = counts[0]

    counts_all = lax.all_to_all(
        jnp.broadcast_to(counts, (groups, 1)), AXES, 0, 0, tiled=True
    ).reshape(groups)

    masks = (4, 2, 2 * net_size, 1, net_size)
    caps = (LINK_CAP, LINK_CAP, LINK_CAP, LINK_CAP, CORE_CAP)
    plan = make_plan(counts_all, masks, caps)
    mine = lax.dynamic_slice(plan, (0, me), (plan.shape[0], 1))[:, 0]
    edges = len(masks)
    send = [mine[e] for e in range(edges)]
    starts = [mine[2 * edges + e] for e in range(edges)]
    places = [mine[3 * edges + e] for e in range(edges)]
    work_count = mine[4 * edges + 1]

    margin = max(caps)
    buffer_rows = max(slot_count + margin, -(-slot_count // CHUNK) * CHUNK)
    padded = jnp.concatenate([states, jnp.zeros((buffer_rows - slot_count, row), states.dtype)])
    pairs = [[(d, d ^ m) for d in range(groups)] for m in masks]
    incoming = [
        lax.ppermute(lax.dynamic_slice(padded, (starts[e], 0), (cap, row)), AXES, pairs[e])
        for e, cap in enumerate(caps)
    ]
    work = padded
    for e in range(edges):
        work = lax.dynamic_update_slice(work, incoming[e], (places[e], 0))

    def step(t, acc):
        rows = lax.dynamic_slice(work, (t * CHUNK, 0), (CHUNK, row))
        logits, values = evaluate(rows, *weights)
        column = jnp.zeros((CHUNK, 1, MOVES), jnp.bfloat16).at[:, 0, 0].set(values)
        return lax.dynamic_update_slice(
            acc, jnp.concatenate([logits, column], axis=1), (t * CHUNK, 0, 0)
        )

    results = lax.fori_loop(
        0,
        (work_count + CHUNK - 1) // CHUNK,
        step,
        jnp.zeros((buffer_rows, FACT + 1, MOVES), jnp.bfloat16),
    )

    final = results
    for e, cap in enumerate(caps):
        back = lax.ppermute(
            lax.dynamic_slice(results, (places[e], 0, 0), (cap, FACT + 1, MOVES)), AXES, pairs[e]
        )
        final = lax.dynamic_update_slice(final, back, (starts[e], 0, 0))
    slot_logits = final[:slot_count, :FACT, :]
    slot_values = final[:slot_count, FACT, 0]
    slot = jnp.arange(slot_count, dtype=jnp.int32)

    alive = slot < own_count
    priors = jnp.where(
        alive[:, None, None], masked_priors(slot_logits, legal, logit_scale), 0.0
    )
    leaf_values = jnp.where(alive, slot_values.astype(jnp.float32), 0.0)
    tree_total = TREE_DEV * groups
    onehot = (owners[:, None] == jnp.arange(tree_total, dtype=jnp.int32)[None, :]).astype(
        jnp.float32
    )
    partial_sums = jnp.dot(leaf_values, onehot, precision=lax.Precision.HIGHEST)
    spread = lax.all_to_all(partial_sums.reshape(groups, TREE_DEV), AXES, 0, 0, tiled=True)
    tree_value = jnp.sum(spread, axis=0)
    return (priors, leaf_values, tree_value)


def solution(mesh):
    in_specs = (
        P(AXES, None),
        P(AXES),
        P(AXES),
        P(AXES, None, None),
        P(),
        P(),
        P(),
        P(),
        P(),
        P(),
        P(),
    )
    out_specs = (P(AXES, None, None), P(AXES), P(AXES))
    return jax.shard_map(body, mesh=mesh, in_specs=in_specs, out_specs=out_specs, check_vma=False)
```

```python
import functools

import jax
import jax.numpy as jnp
from jax import lax
from jax.experimental import pallas as pl
from jax.experimental.pallas import tpu as pltpu
from jax.sharding import PartitionSpec as P

SIDE = 19
BOARD = 361
MOVES = 362
PLANES = 32
FACT = 8
TREE_DEV = 8
AXES = ("search", "net")
CHUNK = 40
PASSES = 3
CORE_CAP = 64
LINK_CAP = 28


def convolve(inputs, kernel):
    return lax.conv_general_dilated(
        inputs,
        kernel,
        (1, 1),
        "SAME",
        dimension_numbers=("NHWC", "HWIO", "NHWC"),
        preferred_element_type=jnp.float32,
    )


def evaluate(batch, in_weight, mid_weight, out_weight, policy_weight, pass_weight, value_weight):
    leaves = batch.shape[0]
    board = batch.reshape(leaves, SIDE, SIDE, PLANES)
    hidden = jax.nn.relu(convolve(board, in_weight)).astype(jnp.bfloat16)
    inner = jax.nn.relu(convolve(hidden, mid_weight[0])).astype(jnp.bfloat16)
    hidden = jax.nn.relu(hidden.astype(jnp.float32) + convolve(inner, out_weight[0])).astype(
        jnp.bfloat16
    )
    cells = jnp.einsum(
        "bhwc,cf->bfhw", hidden, policy_weight, preferred_element_type=jnp.float32
    ).reshape(leaves, FACT, BOARD)
    pooled = jnp.mean(hidden, axis=(1, 2), dtype=jnp.float32)
    passing = jnp.dot(pooled, pass_weight.astype(jnp.float32), precision=lax.Precision.HIGHEST)
    logits = jnp.concatenate([cells, passing[:, :, None]], axis=2).astype(jnp.bfloat16)
    values = jnp.tanh(
        jnp.dot(pooled, value_weight.astype(jnp.float32), precision=lax.Precision.HIGHEST)
    ).astype(jnp.bfloat16)
    return (logits, values)


def masked_priors(logits, legal, logit_scale):
    scaled = logit_scale[None, :, None] * logits.astype(jnp.float32)
    allowed = jnp.concatenate(
        [legal > 0, jnp.ones(legal.shape[:2] + (1,), dtype=jnp.bool_)], axis=2
    )
    peak = jnp.max(jnp.where(allowed, scaled, -1e30), axis=2, keepdims=True)
    weights = jnp.exp(jnp.where(allowed, scaled - peak, -1e30))
    return weights / jnp.sum(weights, axis=2, keepdims=True)


def plan_kernel(masks, caps, counts_ref, out_ref):
    counts_all = counts_ref[...]
    lanes = counts_all.shape[1]
    lane = lax.broadcasted_iota(jnp.int32, counts_all.shape, 1)

    def swap(x, mask):
        up = pltpu.roll(x, mask, 1)
        up_from = pltpu.roll(lane, mask, 1)
        down = pltpu.roll(x, lanes - mask, 1)
        return jnp.where(up_from == (lane ^ mask), up, down)

    flows = [jnp.zeros_like(counts_all) for _ in masks]
    for _ in range(PASSES):
        for e, (mask, cap) in enumerate(zip(masks, caps)):
            sent = sum(flows)
            got = sum(swap(f, m) for f, m in zip(flows, masks))
            load = counts_all - sent + got
            own = counts_all - sent
            move = jnp.right_shift(jnp.maximum(load - swap(load, mask), 0), 1)
            cancel = jnp.minimum(move, swap(flows[e], mask))
            add = jnp.clip(move - cancel, 0, jnp.minimum(cap - flows[e], own))
            flows[e] = flows[e] + add - swap(cancel, mask)
    into = [swap(f, m) for f, m in zip(flows, masks)]
    keep = counts_all - sum(flows)
    starts, places = [], []
    for e in range(len(masks)):
        starts.append(keep + sum(flows[:e]))
        places.append(keep + sum(into[:e]))
    rows = flows + into + starts + places + [keep, keep + sum(into)]
    rows = rows + [jnp.zeros_like(counts_all)] * (out_ref.shape[0] - len(rows))
    out_ref[...] = jnp.concatenate(rows, axis=0)


def make_plan(counts_all, masks, caps):
    groups = counts_all.shape[0]
    lanes = -(-groups // 128) * 128
    padded = jnp.zeros((1, lanes), jnp.int32).at[0, :groups].set(counts_all)
    rows = -(-(4 * len(masks) + 2) // 8) * 8
    return pl.pallas_call(
        functools.partial(plan_kernel, masks, caps),
        out_shape=jax.ShapeDtypeStruct((rows, lanes), jnp.int32),
    )(padded)


def body(
    states,
    counts,
    owners,
    legal,
    in_weight,
    mid_weight,
    out_weight,
    policy_weight,
    pass_weight,
    value_weight,
    logit_scale,
):
    weights = (in_weight, mid_weight, out_weight, policy_weight, pass_weight, value_weight)
    slot_count, row = states.shape
    groups = lax.axis_size(AXES)
    net_size = lax.axis_size("net")
    me = lax.axis_index(AXES)
    own_count = counts[0]

    counts_all = lax.all_to_all(
        jnp.broadcast_to(counts, (groups, 1)), AXES, 0, 0, tiled=True
    ).reshape(groups)

    masks = (4, 2, 2 * net_size, 1, net_size)
    caps = (LINK_CAP, LINK_CAP, LINK_CAP, LINK_CAP, CORE_CAP)
    plan = make_plan(counts_all, masks, caps)
    mine = lax.dynamic_slice(plan, (0, me), (plan.shape[0], 1))[:, 0]
    edges = len(masks)
    send = [mine[e] for e in range(edges)]
    starts = [mine[2 * edges + e] for e in range(edges)]
    places = [mine[3 * edges + e] for e in range(edges)]
    work_count = mine[4 * edges + 1]

    recv = [mine[edges + e] for e in range(edges)]

    margin = max(caps)
    padded = jnp.concatenate([states, jnp.zeros((margin, row), states.dtype)])
    pairs = [[(d, d ^ m) for d in range(groups)] for m in masks]
    incoming = [
        lax.ppermute(lax.dynamic_slice(padded, (starts[e], 0), (cap, row)), AXES, pairs[e])
        for e, cap in enumerate(caps)
    ]

    pool = jnp.concatenate([states] + incoming, axis=0)
    work_rows = -(-slot_count // CHUNK) * CHUNK
    k = jnp.arange(work_rows, dtype=jnp.int32)
    work_idx = k
    base = slot_count
    for e, cap in enumerate(caps):
        inside = (k >= places[e]) & (k < places[e] + recv[e])
        work_idx = jnp.where(inside, base + k - places[e], work_idx)
        base = base + cap
    work_idx = jnp.clip(work_idx, 0, pool.shape[0] - 1)
    flat = FACT * MOVES

    def step(t, carry):
        logits_acc, values_acc = carry
        idx = lax.dynamic_slice(work_idx, (t * CHUNK,), (CHUNK,))
        logits, values = evaluate(jnp.take(pool, idx, axis=0), *weights)
        logits_acc = lax.dynamic_update_slice(
            logits_acc, logits.reshape(CHUNK, flat), (t * CHUNK, 0)
        )
        values_acc = lax.dynamic_update_slice(values_acc, values, (t * CHUNK,))
        return logits_acc, values_acc

    work_logits, work_values = lax.fori_loop(
        0,
        (work_count + CHUNK - 1) // CHUNK,
        step,
        (jnp.zeros((work_rows, flat), jnp.bfloat16), jnp.zeros((work_rows,), jnp.bfloat16)),
    )

    back_logits, back_values = [], []
    for e, cap in enumerate(caps):
        idx = jnp.clip(places[e] + jnp.arange(cap, dtype=jnp.int32), 0, work_rows - 1)
        back_logits.append(lax.ppermute(jnp.take(work_logits, idx, axis=0), AXES, pairs[e]))
        back_values.append(lax.ppermute(jnp.take(work_values, idx, axis=0), AXES, pairs[e]))

    all_logits = jnp.concatenate([work_logits] + back_logits, axis=0)
    all_values = jnp.concatenate([work_values] + back_values, axis=0)
    slot = jnp.arange(slot_count, dtype=jnp.int32)
    pick = slot
    base = work_rows
    for e, cap in enumerate(caps):
        inside = (slot >= starts[e]) & (slot < starts[e] + send[e])
        pick = jnp.where(inside, base + slot - starts[e], pick)
        base = base + cap
    pick = jnp.clip(pick, 0, all_logits.shape[0] - 1)
    slot_logits = jnp.take(all_logits, pick, axis=0).reshape(slot_count, FACT, MOVES)
    slot_values = jnp.take(all_values, pick, axis=0)

    alive = slot < own_count
    priors = jnp.where(
        alive[:, None, None], masked_priors(slot_logits, legal, logit_scale), 0.0
    )
    leaf_values = jnp.where(alive, slot_values.astype(jnp.float32), 0.0)
    tree_total = TREE_DEV * groups
    onehot = (owners[:, None] == jnp.arange(tree_total, dtype=jnp.int32)[None, :]).astype(
        jnp.float32
    )
    partial_sums = jnp.dot(leaf_values, onehot, precision=lax.Precision.HIGHEST)
    spread = lax.all_to_all(partial_sums.reshape(groups, TREE_DEV), AXES, 0, 0, tiled=True)
    tree_value = jnp.sum(spread, axis=0)
    return (priors, leaf_values, tree_value)


def solution(mesh):
    in_specs = (
        P(AXES, None),
        P(AXES),
        P(AXES),
        P(AXES, None, None),
        P(),
        P(),
        P(),
        P(),
        P(),
        P(),
        P(),
    )
    out_specs = (P(AXES, None, None), P(AXES), P(AXES))
    return jax.shard_map(body, mesh=mesh, in_specs=in_specs, out_specs=out_specs, check_vma=False)
```

```python
import functools

import jax
import jax.numpy as jnp
from jax import lax
from jax.experimental import pallas as pl
from jax.experimental.pallas import tpu as pltpu
from jax.sharding import PartitionSpec as P

SIDE = 19
BOARD = 361
MOVES = 362
PLANES = 32
FACT = 8
TREE_DEV = 8
AXES = ("search", "net")
CHUNK = 48
PASSES = 3
CORE_CAP = 64
LINK_CAP = 32


def convolve(inputs, kernel):
    return lax.conv_general_dilated(
        inputs,
        kernel,
        (1, 1),
        "SAME",
        dimension_numbers=("NHWC", "HWIO", "NHWC"),
        preferred_element_type=jnp.float32,
    )


def evaluate(batch, in_weight, mid_weight, out_weight, policy_weight, pass_weight, value_weight):
    leaves = batch.shape[0]
    board = batch.reshape(leaves, SIDE, SIDE, PLANES)
    hidden = jax.nn.relu(convolve(board, in_weight)).astype(jnp.bfloat16)
    inner = jax.nn.relu(convolve(hidden, mid_weight[0])).astype(jnp.bfloat16)
    hidden = jax.nn.relu(hidden.astype(jnp.float32) + convolve(inner, out_weight[0])).astype(
        jnp.bfloat16
    )
    cells = jnp.einsum(
        "bhwc,cf->bfhw", hidden, policy_weight, preferred_element_type=jnp.float32
    ).reshape(leaves, FACT, BOARD)
    pooled = jnp.mean(hidden, axis=(1, 2), dtype=jnp.float32)
    passing = jnp.dot(pooled, pass_weight.astype(jnp.float32), precision=lax.Precision.HIGHEST)
    logits = jnp.concatenate([cells, passing[:, :, None]], axis=2).astype(jnp.bfloat16)
    values = jnp.tanh(
        jnp.dot(pooled, value_weight.astype(jnp.float32), precision=lax.Precision.HIGHEST)
    ).astype(jnp.bfloat16)
    return (logits, values)


def masked_priors(logits, legal, logit_scale):
    scaled = logit_scale[None, :, None] * logits.astype(jnp.float32)
    allowed = jnp.concatenate(
        [legal > 0, jnp.ones(legal.shape[:2] + (1,), dtype=jnp.bool_)], axis=2
    )
    peak = jnp.max(jnp.where(allowed, scaled, -1e30), axis=2, keepdims=True)
    weights = jnp.exp(jnp.where(allowed, scaled - peak, -1e30))
    return weights / jnp.sum(weights, axis=2, keepdims=True)


def plan_kernel(masks, caps, counts_ref, out_ref):
    counts_all = counts_ref[...]
    lanes = counts_all.shape[1]
    lane = lax.broadcasted_iota(jnp.int32, counts_all.shape, 1)

    def swap(x, mask):
        up = pltpu.roll(x, mask, 1)
        up_from = pltpu.roll(lane, mask, 1)
        down = pltpu.roll(x, lanes - mask, 1)
        return jnp.where(up_from == (lane ^ mask), up, down)

    flows = [jnp.zeros_like(counts_all) for _ in masks]
    for _ in range(PASSES):
        for e, (mask, cap) in enumerate(zip(masks, caps)):
            sent = sum(flows)
            got = sum(swap(f, m) for f, m in zip(flows, masks))
            load = counts_all - sent + got
            own = counts_all - sent
            move = jnp.right_shift(jnp.maximum(load - swap(load, mask), 0), 1)
            cancel = jnp.minimum(move, swap(flows[e], mask))
            add = jnp.clip(move - cancel, 0, jnp.minimum(cap - flows[e], own))
            flows[e] = flows[e] + add - swap(cancel, mask)
    into = [swap(f, m) for f, m in zip(flows, masks)]
    keep = counts_all - sum(flows)
    starts, places = [], []
    for e in range(len(masks)):
        starts.append(keep + sum(flows[:e]))
        places.append(keep + sum(into[:e]))
    rows = flows + into + starts + places + [keep, keep + sum(into)]
    rows = rows + [jnp.zeros_like(counts_all)] * (out_ref.shape[0] - len(rows))
    out_ref[...] = jnp.concatenate(rows, axis=0)


def make_plan(counts_all, masks, caps):
    groups = counts_all.shape[0]
    lanes = -(-groups // 128) * 128
    padded = jnp.zeros((1, lanes), jnp.int32).at[0, :groups].set(counts_all)
    rows = -(-(4 * len(masks) + 2) // 8) * 8
    return pl.pallas_call(
        functools.partial(plan_kernel, masks, caps),
        out_shape=jax.ShapeDtypeStruct((rows, lanes), jnp.int32),
    )(padded)


def body(
    states,
    counts,
    owners,
    legal,
    in_weight,
    mid_weight,
    out_weight,
    policy_weight,
    pass_weight,
    value_weight,
    logit_scale,
):
    weights = (in_weight, mid_weight, out_weight, policy_weight, pass_weight, value_weight)
    slot_count, row = states.shape
    groups = lax.axis_size(AXES)
    net_size = lax.axis_size("net")
    me = lax.axis_index(AXES)
    own_count = counts[0]

    counts_all = lax.all_to_all(
        jnp.broadcast_to(counts, (groups, 1)), AXES, 0, 0, tiled=True
    ).reshape(groups)

    masks = (4, 2, 2 * net_size, 1, net_size)
    caps = (LINK_CAP, LINK_CAP, LINK_CAP, LINK_CAP, CORE_CAP)
    plan = make_plan(counts_all, masks, caps)
    mine = lax.dynamic_slice(plan, (0, me), (plan.shape[0], 1))[:, 0]
    edges = len(masks)
    send = [mine[e] for e in range(edges)]
    starts = [mine[2 * edges + e] for e in range(edges)]
    places = [mine[3 * edges + e] for e in range(edges)]
    work_count = mine[4 * edges + 1]

    recv = [mine[edges + e] for e in range(edges)]

    margin = max(caps)
    padded = jnp.concatenate([states, jnp.zeros((margin, row), states.dtype)])
    pairs = [[(d, d ^ m) for d in range(groups)] for m in masks]
    incoming = [
        lax.ppermute(lax.dynamic_slice(padded, (starts[e], 0), (cap, row)), AXES, pairs[e])
        for e, cap in enumerate(caps)
    ]

    pool = jnp.concatenate([states] + incoming, axis=0)
    work_rows = -(-slot_count // CHUNK) * CHUNK
    k = jnp.arange(work_rows, dtype=jnp.int32)
    work_idx = k
    base = slot_count
    for e, cap in enumerate(caps):
        inside = (k >= places[e]) & (k < places[e] + recv[e])
        work_idx = jnp.where(inside, base + k - places[e], work_idx)
        base = base + cap
    work_idx = jnp.clip(work_idx, 0, pool.shape[0] - 1)
    flat = FACT * MOVES

    def step(t, carry):
        logits_acc, values_acc = carry
        idx = lax.dynamic_slice(work_idx, (t * CHUNK,), (CHUNK,))
        logits, values = evaluate(jnp.take(pool, idx, axis=0), *weights)
        logits_acc = lax.dynamic_update_slice(
            logits_acc, logits.reshape(CHUNK, flat), (t * CHUNK, 0)
        )
        values_acc = lax.dynamic_update_slice(values_acc, values, (t * CHUNK,))
        return logits_acc, values_acc

    work_logits, work_values = lax.fori_loop(
        0,
        (work_count + CHUNK - 1) // CHUNK,
        step,
        (jnp.zeros((work_rows, flat), jnp.bfloat16), jnp.zeros((work_rows,), jnp.bfloat16)),
    )

    back_logits, back_values = [], []
    for e, cap in enumerate(caps):
        idx = jnp.clip(places[e] + jnp.arange(cap, dtype=jnp.int32), 0, work_rows - 1)
        back_logits.append(lax.ppermute(jnp.take(work_logits, idx, axis=0), AXES, pairs[e]))
        back_values.append(lax.ppermute(jnp.take(work_values, idx, axis=0), AXES, pairs[e]))

    all_logits = jnp.concatenate([work_logits] + back_logits, axis=0)
    all_values = jnp.concatenate([work_values] + back_values, axis=0)
    slot = jnp.arange(slot_count, dtype=jnp.int32)
    pick = slot
    base = work_rows
    for e, cap in enumerate(caps):
        inside = (slot >= starts[e]) & (slot < starts[e] + send[e])
        pick = jnp.where(inside, base + slot - starts[e], pick)
        base = base + cap
    pick = jnp.clip(pick, 0, all_logits.shape[0] - 1)
    slot_logits = jnp.take(all_logits, pick, axis=0).reshape(slot_count, FACT, MOVES)
    slot_values = jnp.take(all_values, pick, axis=0)

    alive = slot < own_count
    priors = jnp.where(
        alive[:, None, None], masked_priors(slot_logits, legal, logit_scale), 0.0
    )
    leaf_values = jnp.where(alive, slot_values.astype(jnp.float32), 0.0)
    tree_total = TREE_DEV * groups
    onehot = (owners[:, None] == jnp.arange(tree_total, dtype=jnp.int32)[None, :]).astype(
        jnp.float32
    )
    partial_sums = jnp.dot(leaf_values, onehot, precision=lax.Precision.HIGHEST)
    spread = lax.all_to_all(partial_sums.reshape(groups, TREE_DEV), AXES, 0, 0, tiled=True)
    tree_value = jnp.sum(spread, axis=0)
    return (priors, leaf_values, tree_value)


def solution(mesh):
    in_specs = (
        P(AXES, None),
        P(AXES),
        P(AXES),
        P(AXES, None, None),
        P(),
        P(),
        P(),
        P(),
        P(),
        P(),
        P(),
    )
    out_specs = (P(AXES, None, None), P(AXES), P(AXES))
    return jax.shard_map(body, mesh=mesh, in_specs=in_specs, out_specs=out_specs, check_vma=False)
```

```python
import functools

import jax
import jax.numpy as jnp
from jax import lax
from jax.experimental import pallas as pl
from jax.experimental.pallas import tpu as pltpu
from jax.sharding import PartitionSpec as P

SIDE = 19
BOARD = 361
MOVES = 362
PLANES = 32
FACT = 8
TREE_DEV = 8
AXES = ("search", "net")
CHUNK = 40
PASSES = 3
CORE_CAP = 64
LINK_CAP = 32
FAR_CAP = 16


def convolve(inputs, kernel):
    return lax.conv_general_dilated(
        inputs,
        kernel,
        (1, 1),
        "SAME",
        dimension_numbers=("NHWC", "HWIO", "NHWC"),
        preferred_element_type=jnp.float32,
    )


def evaluate(batch, in_weight, mid_weight, out_weight, policy_weight, pass_weight, value_weight):
    leaves = batch.shape[0]
    board = batch.reshape(leaves, SIDE, SIDE, PLANES)
    hidden = jax.nn.relu(convolve(board, in_weight)).astype(jnp.bfloat16)
    inner = jax.nn.relu(convolve(hidden, mid_weight[0])).astype(jnp.bfloat16)
    hidden = jax.nn.relu(hidden.astype(jnp.float32) + convolve(inner, out_weight[0])).astype(
        jnp.bfloat16
    )
    cells = jnp.einsum(
        "bhwc,cf->bfhw", hidden, policy_weight, preferred_element_type=jnp.float32
    ).reshape(leaves, FACT, BOARD)
    pooled = jnp.mean(hidden, axis=(1, 2), dtype=jnp.float32)
    passing = jnp.dot(pooled, pass_weight.astype(jnp.float32), precision=lax.Precision.HIGHEST)
    logits = jnp.concatenate([cells, passing[:, :, None]], axis=2).astype(jnp.bfloat16)
    values = jnp.tanh(
        jnp.dot(pooled, value_weight.astype(jnp.float32), precision=lax.Precision.HIGHEST)
    ).astype(jnp.bfloat16)
    return (logits, values)


def masked_priors(logits, legal, logit_scale):
    scaled = logit_scale[None, :, None] * logits.astype(jnp.float32)
    allowed = jnp.concatenate(
        [legal > 0, jnp.ones(legal.shape[:2] + (1,), dtype=jnp.bool_)], axis=2
    )
    peak = jnp.max(jnp.where(allowed, scaled, -1e30), axis=2, keepdims=True)
    weights = jnp.exp(jnp.where(allowed, scaled - peak, -1e30))
    return weights / jnp.sum(weights, axis=2, keepdims=True)


def plan_kernel(masks, caps, slot_count, work_rows, counts_ref, me_ref, out_ref, idx_ref):
    counts_all = counts_ref[...]
    lanes = counts_all.shape[1]
    lane = lax.broadcasted_iota(jnp.int32, counts_all.shape, 1)

    def swap(x, mask):
        up = pltpu.roll(x, mask, 1)
        up_from = pltpu.roll(lane, mask, 1)
        down = pltpu.roll(x, lanes - mask, 1)
        return jnp.where(up_from == (lane ^ mask), up, down)

    flows = [jnp.zeros_like(counts_all) for _ in masks]
    for _ in range(PASSES):
        for e, (mask, cap) in enumerate(zip(masks, caps)):
            sent = sum(flows)
            got = sum(swap(f, m) for f, m in zip(flows, masks))
            load = counts_all - sent + got
            own = counts_all - sent
            move = jnp.right_shift(jnp.maximum(load - swap(load, mask), 0), 1)
            cancel = jnp.minimum(move, swap(flows[e], mask))
            add = jnp.clip(move - cancel, 0, jnp.minimum(cap - flows[e], own))
            flows[e] = flows[e] + add - swap(cancel, mask)
    into = [swap(f, m) for f, m in zip(flows, masks)]
    keep = counts_all - sum(flows)
    starts, places = [], []
    for e in range(len(masks)):
        starts.append(keep + sum(flows[:e]))
        places.append(keep + sum(into[:e]))
    rows = flows + into + starts + places + [keep, keep + sum(into)]
    rows = rows + [jnp.zeros_like(counts_all)] * (out_ref.shape[0] - len(rows))
    out_ref[...] = jnp.concatenate(rows, axis=0)

    me = me_ref[...]

    def mine(v):
        return jnp.sum(jnp.where(lane == me, v, 0), axis=1, keepdims=True)

    k = lax.broadcasted_iota(jnp.int32, (1, idx_ref.shape[1]), 1)
    work_idx = k
    pick = k
    work_base = slot_count
    pick_base = work_rows
    for e, cap in enumerate(caps):
        place, got_e = mine(places[e]), mine(into[e])
        work_idx = jnp.where((k >= place) & (k < place + got_e), work_base + k - place, work_idx)
        start, sent_e = mine(starts[e]), mine(flows[e])
        pick = jnp.where((k >= start) & (k < start + sent_e), pick_base + k - start, pick)
        work_base = work_base + cap
        pick_base = pick_base + cap
    work_idx = jnp.clip(work_idx, 0, work_base - 1)
    pick = jnp.clip(pick, 0, pick_base - 1)
    idx_ref[...] = jnp.concatenate([work_idx, pick] + [k * 0] * (idx_ref.shape[0] - 2), axis=0)


def make_plan(counts_all, me, masks, caps, slot_count, work_rows):
    groups = counts_all.shape[0]
    lanes = -(-groups // 128) * 128
    padded = jnp.zeros((1, lanes), jnp.int32).at[0, :groups].set(counts_all)
    rows = -(-(4 * len(masks) + 2) // 8) * 8
    width = -(-max(work_rows, slot_count) // 128) * 128
    return pl.pallas_call(
        functools.partial(plan_kernel, masks, caps, slot_count, work_rows),
        out_shape=(
            jax.ShapeDtypeStruct((rows, lanes), jnp.int32),
            jax.ShapeDtypeStruct((8, width), jnp.int32),
        ),
    )(padded, jnp.full((1, lanes), me, jnp.int32))


def body(
    states,
    counts,
    owners,
    legal,
    in_weight,
    mid_weight,
    out_weight,
    policy_weight,
    pass_weight,
    value_weight,
    logit_scale,
):
    weights = (in_weight, mid_weight, out_weight, policy_weight, pass_weight, value_weight)
    slot_count, row = states.shape
    groups = lax.axis_size(AXES)
    net_size = lax.axis_size("net")
    me = lax.axis_index(AXES)
    own_count = counts[0]

    counts_all = lax.all_to_all(
        jnp.broadcast_to(counts, (groups, 1)), AXES, 0, 0, tiled=True
    ).reshape(groups)

    masks = (4, 2, 2 * net_size, 1, net_size)
    caps = (FAR_CAP, LINK_CAP, LINK_CAP, LINK_CAP, CORE_CAP)
    work_rows = -(-slot_count // CHUNK) * CHUNK
    plan, lists = make_plan(counts_all, me, masks, caps, slot_count, work_rows)
    mine = lax.dynamic_slice(plan, (0, me), (plan.shape[0], 1))[:, 0]
    edges = len(masks)
    send = [mine[e] for e in range(edges)]
    starts = [mine[2 * edges + e] for e in range(edges)]
    places = [mine[3 * edges + e] for e in range(edges)]
    work_count = mine[4 * edges + 1]

    recv = [mine[edges + e] for e in range(edges)]

    margin = max(caps)
    padded = jnp.concatenate([states, jnp.zeros((margin, row), states.dtype)])
    pairs = [[(d, d ^ m) for d in range(groups)] for m in masks]
    incoming = [
        lax.ppermute(lax.dynamic_slice(padded, (starts[e], 0), (cap, row)), AXES, pairs[e])
        for e, cap in enumerate(caps)
    ]

    pool = jnp.concatenate([states] + incoming, axis=0)
    work_idx = lists[0, :work_rows]
    flat = FACT * MOVES

    def step(t, carry):
        logits_acc, values_acc = carry
        idx = lax.dynamic_slice(work_idx, (t * CHUNK,), (CHUNK,))
        logits, values = evaluate(jnp.take(pool, idx, axis=0), *weights)
        logits_acc = lax.dynamic_update_slice(
            logits_acc, logits.reshape(CHUNK, flat), (t * CHUNK, 0)
        )
        values_acc = lax.dynamic_update_slice(values_acc, values, (t * CHUNK,))
        return logits_acc, values_acc

    work_logits, work_values = lax.fori_loop(
        0,
        (work_count + CHUNK - 1) // CHUNK,
        step,
        (jnp.zeros((work_rows, flat), jnp.bfloat16), jnp.zeros((work_rows,), jnp.bfloat16)),
    )

    back_logits, back_values = [], []
    for e, cap in enumerate(caps):
        idx = jnp.clip(places[e] + jnp.arange(cap, dtype=jnp.int32), 0, work_rows - 1)
        back_logits.append(lax.ppermute(jnp.take(work_logits, idx, axis=0), AXES, pairs[e]))
        back_values.append(lax.ppermute(jnp.take(work_values, idx, axis=0), AXES, pairs[e]))

    all_logits = jnp.concatenate([work_logits] + back_logits, axis=0)
    all_values = jnp.concatenate([work_values] + back_values, axis=0)
    slot = jnp.arange(slot_count, dtype=jnp.int32)
    pick = lists[1, :slot_count]
    slot_logits = jnp.take(all_logits, pick, axis=0).reshape(slot_count, FACT, MOVES)
    slot_values = jnp.take(all_values, pick, axis=0)

    alive = slot < own_count
    priors = jnp.where(
        alive[:, None, None], masked_priors(slot_logits, legal, logit_scale), 0.0
    )
    leaf_values = jnp.where(alive, slot_values.astype(jnp.float32), 0.0)
    tree_total = TREE_DEV * groups
    onehot = (owners[:, None] == jnp.arange(tree_total, dtype=jnp.int32)[None, :]).astype(
        jnp.float32
    )
    partial_sums = jnp.dot(leaf_values, onehot, precision=lax.Precision.HIGHEST)
    spread = lax.all_to_all(partial_sums.reshape(groups, TREE_DEV), AXES, 0, 0, tiled=True)
    tree_value = jnp.sum(spread, axis=0)
    return (priors, leaf_values, tree_value)


def solution(mesh):
    in_specs = (
        P(AXES, None),
        P(AXES),
        P(AXES),
        P(AXES, None, None),
        P(),
        P(),
        P(),
        P(),
        P(),
        P(),
        P(),
    )
    out_specs = (P(AXES, None, None), P(AXES), P(AXES))
    return jax.shard_map(body, mesh=mesh, in_specs=in_specs, out_specs=out_specs, check_vma=False)
```

```python
import functools

import jax
import jax.numpy as jnp
from jax import lax
from jax.experimental import pallas as pl
from jax.experimental.pallas import tpu as pltpu
from jax.sharding import PartitionSpec as P

SIDE = 19
BOARD = 361
MOVES = 362
PLANES = 32
FACT = 8
TREE_DEV = 8
AXES = ("search", "net")
CHUNK = 40
PASSES = 3
CORE_CAP = 64
LINK_CAP = 32
FAR_CAP = 16


def convolve(inputs, kernel):
    return lax.conv_general_dilated(
        inputs,
        kernel,
        (1, 1),
        "SAME",
        dimension_numbers=("NHWC", "HWIO", "NHWC"),
        preferred_element_type=jnp.float32,
    )


def evaluate(batch, in_weight, mid_weight, out_weight, policy_weight, pass_weight, value_weight):
    leaves = batch.shape[0]
    board = batch.reshape(leaves, SIDE, SIDE, PLANES)
    hidden = jax.nn.relu(convolve(board, in_weight)).astype(jnp.bfloat16)
    inner = jax.nn.relu(convolve(hidden, mid_weight[0])).astype(jnp.bfloat16)
    hidden = jax.nn.relu(hidden.astype(jnp.float32) + convolve(inner, out_weight[0])).astype(
        jnp.bfloat16
    )
    cells = jnp.einsum(
        "bhwc,cf->bfhw", hidden, policy_weight, preferred_element_type=jnp.float32
    ).reshape(leaves, FACT, BOARD)
    pooled = jnp.mean(hidden, axis=(1, 2), dtype=jnp.float32)
    passing = jnp.dot(pooled, pass_weight.astype(jnp.float32), precision=lax.Precision.HIGHEST)
    logits = jnp.concatenate([cells, passing[:, :, None]], axis=2).astype(jnp.bfloat16)
    values = jnp.tanh(
        jnp.dot(pooled, value_weight.astype(jnp.float32), precision=lax.Precision.HIGHEST)
    ).astype(jnp.bfloat16)
    return (logits, values)


def masked_priors(logits, legal, logit_scale):
    scaled = logit_scale[None, :, None] * logits.astype(jnp.float32)
    allowed = jnp.concatenate(
        [legal > 0, jnp.ones(legal.shape[:2] + (1,), dtype=jnp.bool_)], axis=2
    )
    peak = jnp.max(jnp.where(allowed, scaled, -1e30), axis=2, keepdims=True)
    weights = jnp.exp(jnp.where(allowed, scaled - peak, -1e30))
    return weights / jnp.sum(weights, axis=2, keepdims=True)


def plan_kernel(masks, caps, slot_count, work_rows, counts_ref, me_ref, out_ref, idx_ref):
    counts_all = counts_ref[...]
    lanes = counts_all.shape[1]
    lane = lax.broadcasted_iota(jnp.int32, counts_all.shape, 1)

    def swap(x, mask):
        up = pltpu.roll(x, mask, 1)
        up_from = pltpu.roll(lane, mask, 1)
        down = pltpu.roll(x, lanes - mask, 1)
        return jnp.where(up_from == (lane ^ mask), up, down)

    flows = [jnp.zeros_like(counts_all) for _ in masks]
    for _ in range(PASSES):
        for e, (mask, cap) in enumerate(zip(masks, caps)):
            sent = sum(flows)
            got = sum(swap(f, m) for f, m in zip(flows, masks))
            load = counts_all - sent + got
            own = counts_all - sent
            move = jnp.right_shift(jnp.maximum(load - swap(load, mask), 0), 1)
            cancel = jnp.minimum(move, swap(flows[e], mask))
            add = jnp.clip(move - cancel, 0, jnp.minimum(cap - flows[e], own))
            flows[e] = flows[e] + add - swap(cancel, mask)
    into = [swap(f, m) for f, m in zip(flows, masks)]
    keep = counts_all - sum(flows)
    starts, places = [], []
    for e in range(len(masks)):
        starts.append(keep + sum(flows[:e]))
        places.append(keep + sum(into[:e]))
    rows = flows + into + starts + places + [keep, keep + sum(into)]
    rows = rows + [jnp.zeros_like(counts_all)] * (out_ref.shape[0] - len(rows))
    out_ref[...] = jnp.concatenate(rows, axis=0)

    me = me_ref[...]

    def mine(v):
        return jnp.sum(jnp.where(lane == me, v, 0), axis=1, keepdims=True)

    k = lax.broadcasted_iota(jnp.int32, (1, idx_ref.shape[1]), 1)
    work_idx = k
    pick = k
    work_base = slot_count
    pick_base = work_rows + max(caps)
    for e, cap in enumerate(caps):
        place, got_e = mine(places[e]), mine(into[e])
        work_idx = jnp.where((k >= place) & (k < place + got_e), work_base + k - place, work_idx)
        start, sent_e = mine(starts[e]), mine(flows[e])
        pick = jnp.where((k >= start) & (k < start + sent_e), pick_base + k - start, pick)
        work_base = work_base + cap
        pick_base = pick_base + cap
    work_idx = jnp.where(k < mine(keep + sum(into)), jnp.clip(work_idx, 0, work_base - 1), work_base - 1)
    pick = jnp.clip(pick, 0, pick_base - 1)
    idx_ref[...] = jnp.concatenate([work_idx, pick] + [k * 0] * (idx_ref.shape[0] - 2), axis=0)


def make_plan(counts_all, me, masks, caps, slot_count, work_rows):
    groups = counts_all.shape[0]
    lanes = -(-groups // 128) * 128
    padded = jnp.zeros((1, lanes), jnp.int32).at[0, :groups].set(counts_all)
    rows = -(-(4 * len(masks) + 2) // 8) * 8
    width = -(-max(work_rows, slot_count) // 128) * 128
    return pl.pallas_call(
        functools.partial(plan_kernel, masks, caps, slot_count, work_rows),
        out_shape=(
            jax.ShapeDtypeStruct((rows, lanes), jnp.int32),
            jax.ShapeDtypeStruct((8, width), jnp.int32),
        ),
    )(padded, jnp.full((1, lanes), me, jnp.int32))


def body(
    states,
    counts,
    owners,
    legal,
    in_weight,
    mid_weight,
    out_weight,
    policy_weight,
    pass_weight,
    value_weight,
    logit_scale,
):
    weights = (in_weight, mid_weight, out_weight, policy_weight, pass_weight, value_weight)
    slot_count, row = states.shape
    groups = lax.axis_size(AXES)
    net_size = lax.axis_size("net")
    me = lax.axis_index(AXES)
    own_count = counts[0]

    counts_all = lax.all_to_all(
        jnp.broadcast_to(counts, (groups, 1)), AXES, 0, 0, tiled=True
    ).reshape(groups)

    masks = (4, 2, 2 * net_size, 1, net_size)
    caps = (FAR_CAP, LINK_CAP, LINK_CAP, LINK_CAP, CORE_CAP)
    work_rows = -(-slot_count // CHUNK) * CHUNK
    plan, lists = make_plan(counts_all, me, masks, caps, slot_count, work_rows)
    mine = lax.dynamic_slice(plan, (0, me), (plan.shape[0], 1))[:, 0]
    edges = len(masks)
    send = [mine[e] for e in range(edges)]
    starts = [mine[2 * edges + e] for e in range(edges)]
    places = [mine[3 * edges + e] for e in range(edges)]
    work_count = mine[4 * edges + 1]

    recv = [mine[edges + e] for e in range(edges)]

    margin = max(caps)
    padded = jnp.concatenate([states, jnp.zeros((margin, row), states.dtype)])
    pairs = [[(d, d ^ m) for d in range(groups)] for m in masks]
    incoming = [
        lax.ppermute(lax.dynamic_slice(padded, (starts[e], 0), (cap, row)), AXES, pairs[e])
        for e, cap in enumerate(caps)
    ]

    pool = jnp.concatenate([states] + incoming, axis=0)
    work_idx = lists[0, :work_rows]
    flat = FACT * MOVES

    def step(t, carry):
        logits_acc, values_acc = carry
        idx = lax.dynamic_slice(work_idx, (t * CHUNK,), (CHUNK,))
        rows = jnp.take(pool, idx, axis=0, mode="clip", indices_are_sorted=True)
        logits, values = evaluate(rows, *weights)
        logits_acc = lax.dynamic_update_slice(
            logits_acc, logits.reshape(CHUNK, flat), (t * CHUNK, 0)
        )
        values_acc = lax.dynamic_update_slice(values_acc, values, (t * CHUNK,))
        return logits_acc, values_acc

    work_logits, work_values = lax.fori_loop(
        0,
        (work_count + CHUNK - 1) // CHUNK,
        step,
        (
            jnp.zeros((work_rows + margin, flat), jnp.bfloat16),
            jnp.zeros((work_rows + margin,), jnp.bfloat16),
        ),
    )

    back_logits, back_values = [], []
    for e, cap in enumerate(caps):
        window = lax.dynamic_slice(work_logits, (places[e], 0), (cap, flat))
        back_logits.append(lax.ppermute(window, AXES, pairs[e]))
        window = lax.dynamic_slice(work_values, (places[e],), (cap,))
        back_values.append(lax.ppermute(window, AXES, pairs[e]))

    all_logits = jnp.concatenate([work_logits] + back_logits, axis=0)
    all_values = jnp.concatenate([work_values] + back_values, axis=0)
    slot = jnp.arange(slot_count, dtype=jnp.int32)
    pick = lists[1, :slot_count]
    slot_logits = jnp.take(all_logits, pick, axis=0, mode="clip").reshape(slot_count, FACT, MOVES)
    slot_values = jnp.take(all_values, pick, axis=0, mode="clip")

    alive = slot < own_count
    priors = jnp.where(
        alive[:, None, None], masked_priors(slot_logits, legal, logit_scale), 0.0
    )
    leaf_values = jnp.where(alive, slot_values.astype(jnp.float32), 0.0)
    tree_total = TREE_DEV * groups
    onehot = (owners[:, None] == jnp.arange(tree_total, dtype=jnp.int32)[None, :]).astype(
        jnp.float32
    )
    partial_sums = jnp.dot(leaf_values, onehot, precision=lax.Precision.HIGHEST)
    spread = lax.all_to_all(partial_sums.reshape(groups, TREE_DEV), AXES, 0, 0, tiled=True)
    tree_value = jnp.sum(spread, axis=0)
    return (priors, leaf_values, tree_value)


def solution(mesh):
    in_specs = (
        P(AXES, None),
        P(AXES),
        P(AXES),
        P(AXES, None, None),
        P(),
        P(),
        P(),
        P(),
        P(),
        P(),
        P(),
    )
    out_specs = (P(AXES, None, None), P(AXES), P(AXES))
    return jax.shard_map(body, mesh=mesh, in_specs=in_specs, out_specs=out_specs, check_vma=False)
```

```python
import functools

import jax
import jax.numpy as jnp
from jax import lax
from jax.experimental import pallas as pl
from jax.experimental.pallas import tpu as pltpu
from jax.sharding import PartitionSpec as P

SIDE = 19
BOARD = 361
MOVES = 362
PLANES = 32
FACT = 8
TREE_DEV = 8
AXES = ("search", "net")
CHUNK = 40
PASSES = 3
CORE_CAP = 64
LINK_CAP = 32
FAR_CAP = 16


def convolve(inputs, kernel):
    return lax.conv_general_dilated(
        inputs,
        kernel,
        (1, 1),
        "SAME",
        dimension_numbers=("NHWC", "HWIO", "NHWC"),
        preferred_element_type=jnp.float32,
    )


def evaluate(batch, in_weight, mid_weight, out_weight, policy_weight, pass_weight, value_weight):
    leaves = batch.shape[0]
    board = batch.reshape(leaves, SIDE, SIDE, PLANES)
    hidden = jax.nn.relu(convolve(board, in_weight)).astype(jnp.bfloat16)
    inner = jax.nn.relu(convolve(hidden, mid_weight[0])).astype(jnp.bfloat16)
    hidden = jax.nn.relu(hidden.astype(jnp.float32) + convolve(inner, out_weight[0])).astype(
        jnp.bfloat16
    )
    cells = jnp.einsum(
        "bhwc,cf->bfhw", hidden, policy_weight, preferred_element_type=jnp.float32
    ).reshape(leaves, FACT, BOARD)
    pooled = jnp.mean(hidden, axis=(1, 2), dtype=jnp.float32)
    passing = jnp.dot(pooled, pass_weight.astype(jnp.float32), precision=lax.Precision.HIGHEST)
    logits = jnp.concatenate([cells, passing[:, :, None]], axis=2).astype(jnp.bfloat16)
    values = jnp.tanh(
        jnp.dot(pooled, value_weight.astype(jnp.float32), precision=lax.Precision.HIGHEST)
    ).astype(jnp.bfloat16)
    return (logits, values)


def masked_priors(logits, legal, logit_scale):
    scaled = logit_scale[None, :, None] * logits.astype(jnp.float32)
    allowed = jnp.concatenate(
        [legal > 0, jnp.ones(legal.shape[:2] + (1,), dtype=jnp.bool_)], axis=2
    )
    peak = jnp.max(jnp.where(allowed, scaled, -1e30), axis=2, keepdims=True)
    weights = jnp.exp(jnp.where(allowed, scaled - peak, -1e30))
    return weights / jnp.sum(weights, axis=2, keepdims=True)


def plan_kernel(masks, caps, slot_count, work_rows, counts_ref, me_ref, out_ref, idx_ref):
    counts_all = counts_ref[...]
    lanes = counts_all.shape[1]
    lane = lax.broadcasted_iota(jnp.int32, counts_all.shape, 1)

    def swap(x, mask):
        up = pltpu.roll(x, mask, 1)
        up_from = pltpu.roll(lane, mask, 1)
        down = pltpu.roll(x, lanes - mask, 1)
        return jnp.where(up_from == (lane ^ mask), up, down)

    flows = [jnp.zeros_like(counts_all) for _ in masks]
    for _ in range(PASSES):
        for e, (mask, cap) in enumerate(zip(masks, caps)):
            sent = sum(flows)
            got = sum(swap(f, m) for f, m in zip(flows, masks))
            load = counts_all - sent + got
            own = counts_all - sent
            move = jnp.right_shift(jnp.maximum(load - swap(load, mask), 0), 1)
            cancel = jnp.minimum(move, swap(flows[e], mask))
            add = jnp.clip(move - cancel, 0, jnp.minimum(cap - flows[e], own))
            flows[e] = flows[e] + add - swap(cancel, mask)
    into = [swap(f, m) for f, m in zip(flows, masks)]
    keep = counts_all - sum(flows)
    starts, places = [], []
    for e in range(len(masks)):
        starts.append(keep + sum(flows[:e]))
        places.append(keep + sum(into[:e]))
    rows = flows + into + starts + places + [keep, keep + sum(into)]
    rows = rows + [jnp.zeros_like(counts_all)] * (out_ref.shape[0] - len(rows))
    out_ref[...] = jnp.concatenate(rows, axis=0)

    me = me_ref[...]

    def mine(v):
        return jnp.sum(jnp.where(lane == me, v, 0), axis=1, keepdims=True)

    k = lax.broadcasted_iota(jnp.int32, (1, idx_ref.shape[1]), 1)
    work_idx = k
    pick = k
    work_base = slot_count
    pick_base = work_rows + max(caps)
    for e, cap in enumerate(caps):
        place, got_e = mine(places[e]), mine(into[e])
        work_idx = jnp.where((k >= place) & (k < place + got_e), work_base + k - place, work_idx)
        start, sent_e = mine(starts[e]), mine(flows[e])
        pick = jnp.where((k >= start) & (k < start + sent_e), pick_base + k - start, pick)
        work_base = work_base + cap
        pick_base = pick_base + cap
    work_idx = jnp.where(k < mine(keep + sum(into)), jnp.clip(work_idx, 0, work_base - 1), work_base - 1)
    pick = jnp.clip(pick, 0, pick_base - 1)
    idx_ref[...] = jnp.concatenate([work_idx, pick] + [k * 0] * (idx_ref.shape[0] - 2), axis=0)


def make_plan(counts_all, me, masks, caps, slot_count, work_rows):
    groups = counts_all.shape[0]
    lanes = -(-groups // 128) * 128
    padded = jnp.zeros((1, lanes), jnp.int32).at[0, :groups].set(counts_all)
    rows = -(-(4 * len(masks) + 2) // 8) * 8
    width = -(-max(work_rows, slot_count) // 128) * 128
    return pl.pallas_call(
        functools.partial(plan_kernel, masks, caps, slot_count, work_rows),
        out_shape=(
            jax.ShapeDtypeStruct((rows, lanes), jnp.int32),
            jax.ShapeDtypeStruct((8, width), jnp.int32),
        ),
    )(padded, jnp.full((1, lanes), me, jnp.int32))


def body(
    states,
    counts,
    owners,
    legal,
    in_weight,
    mid_weight,
    out_weight,
    policy_weight,
    pass_weight,
    value_weight,
    logit_scale,
):
    weights = (in_weight, mid_weight, out_weight, policy_weight, pass_weight, value_weight)
    slot_count, row = states.shape
    groups = lax.axis_size(AXES)
    net_size = lax.axis_size("net")
    me = lax.axis_index(AXES)
    own_count = counts[0]

    counts_all = lax.all_to_all(
        jnp.broadcast_to(counts, (groups, 1)), AXES, 0, 0, tiled=True
    ).reshape(groups)

    masks = (4, 2, 2 * net_size, 1, net_size)
    caps = (FAR_CAP, LINK_CAP, LINK_CAP, LINK_CAP, CORE_CAP)
    work_rows = -(-slot_count // CHUNK) * CHUNK
    plan, lists = make_plan(counts_all, me, masks, caps, slot_count, work_rows)
    mine = lax.dynamic_slice(plan, (0, me), (plan.shape[0], 1))[:, 0]
    edges = len(masks)
    send = [mine[e] for e in range(edges)]
    starts = [mine[2 * edges + e] for e in range(edges)]
    places = [mine[3 * edges + e] for e in range(edges)]
    work_count = mine[4 * edges + 1]

    recv = [mine[edges + e] for e in range(edges)]

    margin = max(caps)
    padded = jnp.concatenate([states, jnp.zeros((margin, row), states.dtype)])
    pairs = [[(d, d ^ m) for d in range(groups)] for m in masks]
    incoming = [
        lax.ppermute(lax.dynamic_slice(padded, (starts[e], 0), (cap, row)), AXES, pairs[e])
        for e, cap in enumerate(caps)
    ]

    pool = jnp.concatenate([states] + incoming, axis=0)
    work_idx = lists[0, :work_rows]
    flat = FACT * MOVES
    width = -(-(flat + 1) // 128) * 128

    def step(t, acc):
        idx = lax.dynamic_slice(work_idx, (t * CHUNK,), (CHUNK,))
        rows = jnp.take(pool, idx, axis=0, mode="clip", indices_are_sorted=True)
        logits, values = evaluate(rows, *weights)
        packed = jnp.concatenate(
            [
                logits.reshape(CHUNK, flat),
                values[:, None],
                jnp.zeros((CHUNK, width - flat - 1), jnp.bfloat16),
            ],
            axis=1,
        )
        return lax.dynamic_update_slice(acc, packed, (t * CHUNK, 0))

    results = lax.fori_loop(
        0,
        (work_count + CHUNK - 1) // CHUNK,
        step,
        jnp.zeros((work_rows + margin, width), jnp.bfloat16),
    )

    back = [
        lax.ppermute(lax.dynamic_slice(results, (places[e], 0), (cap, width)), AXES, pairs[e])
        for e, cap in enumerate(caps)
    ]

    gathered = jnp.take(
        jnp.concatenate([results] + back, axis=0), lists[1, :slot_count], axis=0, mode="clip"
    )
    slot_logits = gathered[:, :flat].reshape(slot_count, FACT, MOVES)
    slot_values = gathered[:, flat]
    slot = jnp.arange(slot_count, dtype=jnp.int32)

    alive = slot < own_count
    priors = jnp.where(
        alive[:, None, None], masked_priors(slot_logits, legal, logit_scale), 0.0
    )
    leaf_values = jnp.where(alive, slot_values.astype(jnp.float32), 0.0)
    tree_total = TREE_DEV * groups
    onehot = (owners[:, None] == jnp.arange(tree_total, dtype=jnp.int32)[None, :]).astype(
        jnp.float32
    )
    partial_sums = jnp.dot(leaf_values, onehot, precision=lax.Precision.HIGHEST)
    spread = lax.all_to_all(partial_sums.reshape(groups, TREE_DEV), AXES, 0, 0, tiled=True)
    tree_value = jnp.sum(spread, axis=0)
    return (priors, leaf_values, tree_value)


def solution(mesh):
    in_specs = (
        P(AXES, None),
        P(AXES),
        P(AXES),
        P(AXES, None, None),
        P(),
        P(),
        P(),
        P(),
        P(),
        P(),
        P(),
    )
    out_specs = (P(AXES, None, None), P(AXES), P(AXES))
    return jax.shard_map(body, mesh=mesh, in_specs=in_specs, out_specs=out_specs, check_vma=False)
```

```python
import functools

import jax
import jax.numpy as jnp
from jax import lax
from jax.experimental import pallas as pl
from jax.experimental.pallas import tpu as pltpu
from jax.sharding import PartitionSpec as P

SIDE = 19
BOARD = 361
MOVES = 362
PLANES = 32
FACT = 8
TREE_DEV = 8
AXES = ("search", "net")
CHUNK = 40
PASSES = 3
CORE_CAP = 64
LINK_CAP = 32
FAR_CAP = 16


def convolve(inputs, kernel):
    return lax.conv_general_dilated(
        inputs,
        kernel,
        (1, 1),
        "SAME",
        dimension_numbers=("NHWC", "HWIO", "NHWC"),
        preferred_element_type=jnp.float32,
    )


def evaluate(batch, in_weight, mid_weight, out_weight, policy_weight, pass_weight, value_weight):
    leaves = batch.shape[0]
    board = batch.reshape(leaves, SIDE, SIDE, PLANES)
    hidden = jax.nn.relu(convolve(board, in_weight)).astype(jnp.bfloat16)
    inner = jax.nn.relu(convolve(hidden, mid_weight[0])).astype(jnp.bfloat16)
    hidden = jax.nn.relu(hidden.astype(jnp.float32) + convolve(inner, out_weight[0])).astype(
        jnp.bfloat16
    )
    cells = jnp.einsum(
        "bhwc,cf->bfhw", hidden, policy_weight, preferred_element_type=jnp.float32
    ).reshape(leaves, FACT, BOARD)
    pooled = jnp.mean(hidden, axis=(1, 2), dtype=jnp.float32)
    passing = jnp.dot(pooled, pass_weight.astype(jnp.float32), precision=lax.Precision.HIGHEST)
    logits = jnp.concatenate([cells, passing[:, :, None]], axis=2).astype(jnp.bfloat16)
    values = jnp.tanh(
        jnp.dot(pooled, value_weight.astype(jnp.float32), precision=lax.Precision.HIGHEST)
    ).astype(jnp.bfloat16)
    return (logits, values)


def masked_priors(logits, legal, logit_scale):
    scaled = logit_scale[None, :, None] * logits.astype(jnp.float32)
    allowed = jnp.concatenate(
        [legal > 0, jnp.ones(legal.shape[:2] + (1,), dtype=jnp.bool_)], axis=2
    )
    peak = jnp.max(jnp.where(allowed, scaled, -1e30), axis=2, keepdims=True)
    weights = jnp.exp(jnp.where(allowed, scaled - peak, -1e30))
    return weights / jnp.sum(weights, axis=2, keepdims=True)


def plan_kernel(masks, caps, slot_count, work_rows, counts_ref, me_ref, out_ref, idx_ref):
    counts_all = counts_ref[...]
    lanes = counts_all.shape[1]
    lane = lax.broadcasted_iota(jnp.int32, counts_all.shape, 1)

    def swap(x, mask):
        up = pltpu.roll(x, mask, 1)
        up_from = pltpu.roll(lane, mask, 1)
        down = pltpu.roll(x, lanes - mask, 1)
        return jnp.where(up_from == (lane ^ mask), up, down)

    flows = [jnp.zeros_like(counts_all) for _ in masks]
    for _ in range(PASSES):
        for e, (mask, cap) in enumerate(zip(masks, caps)):
            sent = sum(flows)
            got = sum(swap(f, m) for f, m in zip(flows, masks))
            load = counts_all - sent + got
            own = counts_all - sent
            move = jnp.right_shift(jnp.maximum(load - swap(load, mask), 0), 1)
            cancel = jnp.minimum(move, swap(flows[e], mask))
            add = jnp.clip(move - cancel, 0, jnp.minimum(cap - flows[e], own))
            flows[e] = flows[e] + add - swap(cancel, mask)
    into = [swap(f, m) for f, m in zip(flows, masks)]
    keep = counts_all - sum(flows)
    starts, places = [], []
    for e in range(len(masks)):
        starts.append(keep + sum(flows[:e]))
        places.append(keep + sum(into[:e]))
    rows = flows + into + starts + places + [keep, keep + sum(into)]
    rows = rows + [jnp.zeros_like(counts_all)] * (out_ref.shape[0] - len(rows))
    out_ref[...] = jnp.concatenate(rows, axis=0)

    me = me_ref[...]

    def mine(v):
        return jnp.sum(jnp.where(lane == me, v, 0), axis=1, keepdims=True)

    k = lax.broadcasted_iota(jnp.int32, (1, idx_ref.shape[1]), 1)
    work_idx = k
    pick = k
    work_base = slot_count
    pick_base = work_rows + max(caps)
    for e, cap in enumerate(caps):
        place, got_e = mine(places[e]), mine(into[e])
        work_idx = jnp.where((k >= place) & (k < place + got_e), work_base + k - place, work_idx)
        start, sent_e = mine(starts[e]), mine(flows[e])
        pick = jnp.where((k >= start) & (k < start + sent_e), pick_base + k - start, pick)
        work_base = work_base + cap
        pick_base = pick_base + cap
    work_idx = jnp.where(k < mine(keep + sum(into)), jnp.clip(work_idx, 0, work_base - 1), work_base - 1)
    pick = jnp.clip(pick, 0, pick_base - 1)
    send_idx = k * 0
    back_idx = k * 0
    seg = 0
    for e, cap in enumerate(caps):
        inside = (k >= seg) & (k < seg + cap)
        send_idx = jnp.where(inside, mine(starts[e]) + k - seg, send_idx)
        back_idx = jnp.where(inside, mine(places[e]) + k - seg, back_idx)
        seg = seg + cap
    send_idx = jnp.clip(send_idx, 0, slot_count - 1)
    back_idx = jnp.clip(back_idx, 0, work_rows + max(caps) - 1)
    rows = [work_idx, pick, send_idx, back_idx]
    idx_ref[...] = jnp.concatenate(rows + [k * 0] * (idx_ref.shape[0] - len(rows)), axis=0)


def make_plan(counts_all, me, masks, caps, slot_count, work_rows):
    groups = counts_all.shape[0]
    lanes = -(-groups // 128) * 128
    padded = jnp.zeros((1, lanes), jnp.int32).at[0, :groups].set(counts_all)
    rows = -(-(4 * len(masks) + 2) // 8) * 8
    width = -(-max(work_rows, slot_count, sum(caps)) // 128) * 128
    return pl.pallas_call(
        functools.partial(plan_kernel, masks, caps, slot_count, work_rows),
        out_shape=(
            jax.ShapeDtypeStruct((rows, lanes), jnp.int32),
            jax.ShapeDtypeStruct((8, width), jnp.int32),
        ),
    )(padded, jnp.full((1, lanes), me, jnp.int32))


def body(
    states,
    counts,
    owners,
    legal,
    in_weight,
    mid_weight,
    out_weight,
    policy_weight,
    pass_weight,
    value_weight,
    logit_scale,
):
    weights = (in_weight, mid_weight, out_weight, policy_weight, pass_weight, value_weight)
    slot_count, row = states.shape
    groups = lax.axis_size(AXES)
    net_size = lax.axis_size("net")
    me = lax.axis_index(AXES)
    own_count = counts[0]

    counts_all = lax.all_to_all(
        jnp.broadcast_to(counts, (groups, 1)), AXES, 0, 0, tiled=True
    ).reshape(groups)

    masks = (4, 2, 2 * net_size, 1, net_size)
    caps = (FAR_CAP, LINK_CAP, LINK_CAP, LINK_CAP, CORE_CAP)
    work_rows = -(-slot_count // CHUNK) * CHUNK
    plan, lists = make_plan(counts_all, me, masks, caps, slot_count, work_rows)
    edges = len(masks)
    work_count = lax.dynamic_slice(plan, (4 * edges + 1, me), (1, 1))[0, 0]
    segments = []
    seg = 0
    for cap in caps:
        segments.append((seg, cap))
        seg += cap

    margin = max(caps)
    pairs = [[(d, d ^ m) for d in range(groups)] for m in masks]
    outgoing = jnp.take(states, lists[2, :seg], axis=0, mode="clip")
    incoming = [
        lax.ppermute(outgoing[first : first + cap], AXES, pairs[e])
        for e, (first, cap) in enumerate(segments)
    ]

    pool = jnp.concatenate([states] + incoming, axis=0)
    work_idx = lists[0, :work_rows]
    flat = FACT * MOVES
    width = -(-(flat + 1) // 128) * 128

    def step(t, acc):
        idx = lax.dynamic_slice(work_idx, (t * CHUNK,), (CHUNK,))
        rows = jnp.take(pool, idx, axis=0, mode="clip", indices_are_sorted=True)
        logits, values = evaluate(rows, *weights)
        packed = jnp.concatenate(
            [
                logits.reshape(CHUNK, flat),
                values[:, None],
                jnp.zeros((CHUNK, width - flat - 1), jnp.bfloat16),
            ],
            axis=1,
        )
        return lax.dynamic_update_slice(acc, packed, (t * CHUNK, 0))

    results = lax.fori_loop(
        0,
        (work_count + CHUNK - 1) // CHUNK,
        step,
        jnp.zeros((work_rows + margin, width), jnp.bfloat16),
    )

    returned = jnp.take(results, lists[3, :seg], axis=0, mode="clip")
    back = [
        lax.ppermute(returned[first : first + cap], AXES, pairs[e])
        for e, (first, cap) in enumerate(segments)
    ]

    gathered = jnp.take(
        jnp.concatenate([results] + back, axis=0), lists[1, :slot_count], axis=0, mode="clip"
    )
    slot_logits = gathered[:, :flat].reshape(slot_count, FACT, MOVES)
    slot_values = gathered[:, flat]
    slot = jnp.arange(slot_count, dtype=jnp.int32)

    alive = slot < own_count
    priors = jnp.where(
        alive[:, None, None], masked_priors(slot_logits, legal, logit_scale), 0.0
    )
    leaf_values = jnp.where(alive, slot_values.astype(jnp.float32), 0.0)
    tree_total = TREE_DEV * groups
    onehot = (owners[:, None] == jnp.arange(tree_total, dtype=jnp.int32)[None, :]).astype(
        jnp.float32
    )
    partial_sums = jnp.dot(leaf_values, onehot, precision=lax.Precision.HIGHEST)
    spread = lax.all_to_all(partial_sums.reshape(groups, TREE_DEV), AXES, 0, 0, tiled=True)
    tree_value = jnp.sum(spread, axis=0)
    return (priors, leaf_values, tree_value)


def solution(mesh):
    in_specs = (
        P(AXES, None),
        P(AXES),
        P(AXES),
        P(AXES, None, None),
        P(),
        P(),
        P(),
        P(),
        P(),
        P(),
        P(),
    )
    out_specs = (P(AXES, None, None), P(AXES), P(AXES))
    return jax.shard_map(body, mesh=mesh, in_specs=in_specs, out_specs=out_specs, check_vma=False)
```

```python
import functools

import jax
import jax.numpy as jnp
from jax import lax
from jax.experimental import pallas as pl
from jax.experimental.pallas import tpu as pltpu
from jax.sharding import PartitionSpec as P

SIDE = 19
BOARD = 361
MOVES = 362
PLANES = 32
FACT = 8
TREE_DEV = 8
AXES = ("search", "net")
CHUNK = 40
PASSES = 5
CORE_CAP = 64
LINK_CAP = 32
FAR_CAP = 32


def convolve(inputs, kernel):
    return lax.conv_general_dilated(
        inputs,
        kernel,
        (1, 1),
        "SAME",
        dimension_numbers=("NHWC", "HWIO", "NHWC"),
        preferred_element_type=jnp.float32,
    )


def evaluate(batch, in_weight, mid_weight, out_weight, policy_weight, pass_weight, value_weight):
    leaves = batch.shape[0]
    board = batch.reshape(leaves, SIDE, SIDE, PLANES)
    hidden = jax.nn.relu(convolve(board, in_weight)).astype(jnp.bfloat16)
    inner = jax.nn.relu(convolve(hidden, mid_weight[0])).astype(jnp.bfloat16)
    hidden = jax.nn.relu(hidden.astype(jnp.float32) + convolve(inner, out_weight[0])).astype(
        jnp.bfloat16
    )
    cells = jnp.einsum(
        "bhwc,cf->bfhw", hidden, policy_weight, preferred_element_type=jnp.float32
    ).reshape(leaves, FACT, BOARD)
    pooled = jnp.mean(hidden, axis=(1, 2), dtype=jnp.float32)
    passing = jnp.dot(pooled, pass_weight.astype(jnp.float32), precision=lax.Precision.HIGHEST)
    logits = jnp.concatenate([cells, passing[:, :, None]], axis=2).astype(jnp.bfloat16)
    values = jnp.tanh(
        jnp.dot(pooled, value_weight.astype(jnp.float32), precision=lax.Precision.HIGHEST)
    ).astype(jnp.bfloat16)
    return (logits, values)


def masked_priors(logits, legal, logit_scale):
    scaled = logit_scale[None, :, None] * logits.astype(jnp.float32)
    allowed = jnp.concatenate(
        [legal > 0, jnp.ones(legal.shape[:2] + (1,), dtype=jnp.bool_)], axis=2
    )
    peak = jnp.max(jnp.where(allowed, scaled, -1e30), axis=2, keepdims=True)
    weights = jnp.exp(jnp.where(allowed, scaled - peak, -1e30))
    return weights / jnp.sum(weights, axis=2, keepdims=True)


def plan_kernel(masks, caps, slot_count, work_rows, counts_ref, me_ref, out_ref, idx_ref):
    counts_all = counts_ref[...]
    lanes = counts_all.shape[1]
    lane = lax.broadcasted_iota(jnp.int32, counts_all.shape, 1)

    def swap(x, mask):
        up = pltpu.roll(x, mask, 1)
        up_from = pltpu.roll(lane, mask, 1)
        down = pltpu.roll(x, lanes - mask, 1)
        return jnp.where(up_from == (lane ^ mask), up, down)

    flows = [jnp.zeros_like(counts_all) for _ in masks]
    for _ in range(PASSES):
        for e, (mask, cap) in enumerate(zip(masks, caps)):
            sent = sum(flows)
            got = sum(swap(f, m) for f, m in zip(flows, masks))
            load = counts_all - sent + got
            own = counts_all - sent
            move = jnp.right_shift(jnp.maximum(load - swap(load, mask), 0), 1)
            cancel = jnp.minimum(move, swap(flows[e], mask))
            add = jnp.clip(move - cancel, 0, jnp.minimum(cap - flows[e], own))
            flows[e] = flows[e] + add - swap(cancel, mask)
    into = [swap(f, m) for f, m in zip(flows, masks)]
    keep = counts_all - sum(flows)
    starts, places = [], []
    for e in range(len(masks)):
        starts.append(keep + sum(flows[:e]))
        places.append(keep + sum(into[:e]))
    rows = flows + into + starts + places + [keep, keep + sum(into)]
    rows = rows + [jnp.zeros_like(counts_all)] * (out_ref.shape[0] - len(rows))
    out_ref[...] = jnp.concatenate(rows, axis=0)

    me = me_ref[...]

    def mine(v):
        return jnp.sum(jnp.where(lane == me, v, 0), axis=1, keepdims=True)

    k = lax.broadcasted_iota(jnp.int32, (1, idx_ref.shape[1]), 1)
    work_idx = k
    pick = k
    work_base = slot_count
    pick_base = work_rows + max(caps)
    for e, cap in enumerate(caps):
        place, got_e = mine(places[e]), mine(into[e])
        work_idx = jnp.where((k >= place) & (k < place + got_e), work_base + k - place, work_idx)
        start, sent_e = mine(starts[e]), mine(flows[e])
        pick = jnp.where((k >= start) & (k < start + sent_e), pick_base + k - start, pick)
        work_base = work_base + cap
        pick_base = pick_base + cap
    work_idx = jnp.where(k < mine(keep + sum(into)), jnp.clip(work_idx, 0, work_base - 1), work_base - 1)
    pick = jnp.clip(pick, 0, pick_base - 1)
    send_idx = k * 0
    back_idx = k * 0
    seg = 0
    for e, cap in enumerate(caps):
        inside = (k >= seg) & (k < seg + cap)
        send_idx = jnp.where(inside, mine(starts[e]) + k - seg, send_idx)
        back_idx = jnp.where(inside, mine(places[e]) + k - seg, back_idx)
        seg = seg + cap
    send_idx = jnp.clip(send_idx, 0, slot_count - 1)
    back_idx = jnp.clip(back_idx, 0, work_rows + max(caps) - 1)
    rows = [work_idx, pick, send_idx, back_idx]
    idx_ref[...] = jnp.concatenate(rows + [k * 0] * (idx_ref.shape[0] - len(rows)), axis=0)


def make_plan(counts_all, me, masks, caps, slot_count, work_rows):
    groups = counts_all.shape[0]
    lanes = -(-groups // 128) * 128
    padded = jnp.zeros((1, lanes), jnp.int32).at[0, :groups].set(counts_all)
    rows = -(-(4 * len(masks) + 2) // 8) * 8
    width = -(-max(work_rows, slot_count, sum(caps)) // 128) * 128
    return pl.pallas_call(
        functools.partial(plan_kernel, masks, caps, slot_count, work_rows),
        out_shape=(
            jax.ShapeDtypeStruct((rows, lanes), jnp.int32),
            jax.ShapeDtypeStruct((8, width), jnp.int32),
        ),
    )(padded, jnp.full((1, lanes), me, jnp.int32))


def body(
    states,
    counts,
    owners,
    legal,
    in_weight,
    mid_weight,
    out_weight,
    policy_weight,
    pass_weight,
    value_weight,
    logit_scale,
):
    weights = (in_weight, mid_weight, out_weight, policy_weight, pass_weight, value_weight)
    slot_count, row = states.shape
    groups = lax.axis_size(AXES)
    net_size = lax.axis_size("net")
    me = lax.axis_index(AXES)
    own_count = counts[0]

    counts_all = lax.all_to_all(
        jnp.broadcast_to(counts, (groups, 1)), AXES, 0, 0, tiled=True
    ).reshape(groups)

    masks = (4, 2, 2 * net_size, 1, net_size)
    caps = (FAR_CAP, LINK_CAP, LINK_CAP, LINK_CAP, CORE_CAP)
    work_rows = -(-slot_count // CHUNK) * CHUNK
    plan, lists = make_plan(counts_all, me, masks, caps, slot_count, work_rows)
    edges = len(masks)
    work_count = lax.dynamic_slice(plan, (4 * edges + 1, me), (1, 1))[0, 0]
    segments = []
    seg = 0
    for cap in caps:
        segments.append((seg, cap))
        seg += cap

    margin = max(caps)
    pairs = [[(d, d ^ m) for d in range(groups)] for m in masks]
    outgoing = jnp.take(states, lists[2, :seg], axis=0, mode="clip")
    incoming = [
        lax.ppermute(outgoing[first : first + cap], AXES, pairs[e])
        for e, (first, cap) in enumerate(segments)
    ]

    pool = jnp.concatenate([states] + incoming, axis=0)
    work_idx = lists[0, :work_rows]
    flat = FACT * MOVES
    width = -(-(flat + 1) // 128) * 128

    def step(t, acc):
        idx = lax.dynamic_slice(work_idx, (t * CHUNK,), (CHUNK,))
        rows = jnp.take(pool, idx, axis=0, mode="clip", indices_are_sorted=True)
        logits, values = evaluate(rows, *weights)
        packed = jnp.concatenate(
            [
                logits.reshape(CHUNK, flat),
                values[:, None],
                jnp.zeros((CHUNK, width - flat - 1), jnp.bfloat16),
            ],
            axis=1,
        )
        return lax.dynamic_update_slice(acc, packed, (t * CHUNK, 0))

    results = lax.fori_loop(
        0,
        (work_count + CHUNK - 1) // CHUNK,
        step,
        jnp.zeros((work_rows + margin, width), jnp.bfloat16),
    )

    returned = jnp.take(results, lists[3, :seg], axis=0, mode="clip")
    back = [
        lax.ppermute(returned[first : first + cap], AXES, pairs[e])
        for e, (first, cap) in enumerate(segments)
    ]

    gathered = jnp.take(
        jnp.concatenate([results] + back, axis=0), lists[1, :slot_count], axis=0, mode="clip"
    )
    slot_logits = gathered[:, :flat].reshape(slot_count, FACT, MOVES)
    slot_values = gathered[:, flat]
    slot = jnp.arange(slot_count, dtype=jnp.int32)

    alive = slot < own_count
    priors = jnp.where(
        alive[:, None, None], masked_priors(slot_logits, legal, logit_scale), 0.0
    )
    leaf_values = jnp.where(alive, slot_values.astype(jnp.float32), 0.0)
    tree_total = TREE_DEV * groups
    onehot = (owners[:, None] == jnp.arange(tree_total, dtype=jnp.int32)[None, :]).astype(
        jnp.float32
    )
    partial_sums = jnp.dot(leaf_values, onehot, precision=lax.Precision.HIGHEST)
    spread = lax.all_to_all(partial_sums.reshape(groups, TREE_DEV), AXES, 0, 0, tiled=True)
    tree_value = jnp.sum(spread, axis=0)
    return (priors, leaf_values, tree_value)


def solution(mesh):
    in_specs = (
        P(AXES, None),
        P(AXES),
        P(AXES),
        P(AXES, None, None),
        P(),
        P(),
        P(),
        P(),
        P(),
        P(),
        P(),
    )
    out_specs = (P(AXES, None, None), P(AXES), P(AXES))
    return jax.shard_map(body, mesh=mesh, in_specs=in_specs, out_specs=out_specs, check_vma=False)
```

```python
import functools

import jax
import jax.numpy as jnp
from jax import lax
from jax.experimental import pallas as pl
from jax.experimental.pallas import tpu as pltpu
from jax.sharding import PartitionSpec as P

SIDE = 19
BOARD = 361
MOVES = 362
PLANES = 32
FACT = 8
TREE_DEV = 8
AXES = ("search", "net")
CHUNK = 40
PASSES = 5
CORE_CAP = 64
LINK_CAP = 32
FAR_CAP = 16


def convolve(inputs, kernel):
    return lax.conv_general_dilated(
        inputs,
        kernel,
        (1, 1),
        "SAME",
        dimension_numbers=("NHWC", "HWIO", "NHWC"),
        preferred_element_type=jnp.float32,
    )


def evaluate(batch, in_weight, mid_weight, out_weight, policy_weight, pass_weight, value_weight):
    leaves = batch.shape[0]
    board = batch.reshape(leaves, SIDE, SIDE, PLANES)
    hidden = jax.nn.relu(convolve(board, in_weight)).astype(jnp.bfloat16)
    inner = jax.nn.relu(convolve(hidden, mid_weight[0])).astype(jnp.bfloat16)
    hidden = jax.nn.relu(hidden.astype(jnp.float32) + convolve(inner, out_weight[0])).astype(
        jnp.bfloat16
    )
    cells = jnp.einsum(
        "bhwc,cf->bfhw", hidden, policy_weight, preferred_element_type=jnp.float32
    ).reshape(leaves, FACT, BOARD)
    pooled = jnp.mean(hidden, axis=(1, 2), dtype=jnp.float32)
    passing = jnp.dot(pooled, pass_weight.astype(jnp.float32), precision=lax.Precision.HIGHEST)
    logits = jnp.concatenate([cells, passing[:, :, None]], axis=2).astype(jnp.bfloat16)
    values = jnp.tanh(
        jnp.dot(pooled, value_weight.astype(jnp.float32), precision=lax.Precision.HIGHEST)
    ).astype(jnp.bfloat16)
    return (logits, values)


def masked_priors(logits, legal, logit_scale):
    scaled = logit_scale[None, :, None] * logits.astype(jnp.float32)
    allowed = jnp.concatenate(
        [legal > 0, jnp.ones(legal.shape[:2] + (1,), dtype=jnp.bool_)], axis=2
    )
    peak = jnp.max(jnp.where(allowed, scaled, -1e30), axis=2, keepdims=True)
    weights = jnp.exp(jnp.where(allowed, scaled - peak, -1e30))
    return weights / jnp.sum(weights, axis=2, keepdims=True)


def plan_kernel(masks, caps, slot_count, work_rows, counts_ref, me_ref, out_ref, idx_ref):
    counts_all = counts_ref[...]
    lanes = counts_all.shape[1]
    lane = lax.broadcasted_iota(jnp.int32, counts_all.shape, 1)

    def swap(x, mask):
        up = pltpu.roll(x, mask, 1)
        up_from = pltpu.roll(lane, mask, 1)
        down = pltpu.roll(x, lanes - mask, 1)
        return jnp.where(up_from == (lane ^ mask), up, down)

    flows = [jnp.zeros_like(counts_all) for _ in masks]
    for _ in range(PASSES):
        for e, (mask, cap) in enumerate(zip(masks, caps)):
            sent = sum(flows)
            got = sum(swap(f, m) for f, m in zip(flows, masks))
            load = counts_all - sent + got
            own = counts_all - sent
            move = jnp.right_shift(jnp.maximum(load - swap(load, mask), 0), 1)
            cancel = jnp.minimum(move, swap(flows[e], mask))
            add = jnp.clip(move - cancel, 0, jnp.minimum(cap - flows[e], own))
            flows[e] = flows[e] + add - swap(cancel, mask)
    into = [swap(f, m) for f, m in zip(flows, masks)]
    keep = counts_all - sum(flows)
    starts, places = [], []
    for e in range(len(masks)):
        starts.append(keep + sum(flows[:e]))
        places.append(keep + sum(into[:e]))
    rows = flows + into + starts + places + [keep, keep + sum(into)]
    rows = rows + [jnp.zeros_like(counts_all)] * (out_ref.shape[0] - len(rows))
    out_ref[...] = jnp.concatenate(rows, axis=0)

    me = me_ref[...]

    def mine(v):
        return jnp.sum(jnp.where(lane == me, v, 0), axis=1, keepdims=True)

    k = lax.broadcasted_iota(jnp.int32, (1, idx_ref.shape[1]), 1)
    work_idx = k
    pick = k
    work_base = slot_count
    pick_base = work_rows + max(caps)
    for e, cap in enumerate(caps):
        place, got_e = mine(places[e]), mine(into[e])
        work_idx = jnp.where((k >= place) & (k < place + got_e), work_base + k - place, work_idx)
        start, sent_e = mine(starts[e]), mine(flows[e])
        pick = jnp.where((k >= start) & (k < start + sent_e), pick_base + k - start, pick)
        work_base = work_base + cap
        pick_base = pick_base + cap
    work_idx = jnp.where(k < mine(keep + sum(into)), jnp.clip(work_idx, 0, work_base - 1), work_base - 1)
    pick = jnp.clip(pick, 0, pick_base - 1)
    idx_ref[...] = jnp.concatenate([work_idx, pick] + [k * 0] * (idx_ref.shape[0] - 2), axis=0)


def make_plan(counts_all, me, masks, caps, slot_count, work_rows):
    groups = counts_all.shape[0]
    lanes = -(-groups // 128) * 128
    padded = jnp.zeros((1, lanes), jnp.int32).at[0, :groups].set(counts_all)
    rows = -(-(4 * len(masks) + 2) // 8) * 8
    width = -(-max(work_rows, slot_count) // 128) * 128
    return pl.pallas_call(
        functools.partial(plan_kernel, masks, caps, slot_count, work_rows),
        out_shape=(
            jax.ShapeDtypeStruct((rows, lanes), jnp.int32),
            jax.ShapeDtypeStruct((8, width), jnp.int32),
        ),
    )(padded, jnp.full((1, lanes), me, jnp.int32))


def body(
    states,
    counts,
    owners,
    legal,
    in_weight,
    mid_weight,
    out_weight,
    policy_weight,
    pass_weight,
    value_weight,
    logit_scale,
):
    weights = (in_weight, mid_weight, out_weight, policy_weight, pass_weight, value_weight)
    slot_count, row = states.shape
    groups = lax.axis_size(AXES)
    net_size = lax.axis_size("net")
    me = lax.axis_index(AXES)
    own_count = counts[0]

    counts_all = lax.all_to_all(
        jnp.broadcast_to(counts, (groups, 1)), AXES, 0, 0, tiled=True
    ).reshape(groups)

    masks = (4, 2, 2 * net_size, 1, net_size)
    caps = (FAR_CAP, LINK_CAP, LINK_CAP, LINK_CAP, CORE_CAP)
    work_rows = -(-slot_count // CHUNK) * CHUNK
    plan, lists = make_plan(counts_all, me, masks, caps, slot_count, work_rows)
    mine = lax.dynamic_slice(plan, (0, me), (plan.shape[0], 1))[:, 0]
    edges = len(masks)
    send = [mine[e] for e in range(edges)]
    starts = [mine[2 * edges + e] for e in range(edges)]
    places = [mine[3 * edges + e] for e in range(edges)]
    work_count = mine[4 * edges + 1]

    recv = [mine[edges + e] for e in range(edges)]

    margin = max(caps)
    padded = jnp.concatenate([states, jnp.zeros((margin, row), states.dtype)])
    pairs = [[(d, d ^ m) for d in range(groups)] for m in masks]
    incoming = [
        lax.ppermute(lax.dynamic_slice(padded, (starts[e], 0), (cap, row)), AXES, pairs[e])
        for e, cap in enumerate(caps)
    ]

    pool = jnp.concatenate([states] + incoming, axis=0)
    work_idx = lists[0, :work_rows]
    flat = FACT * MOVES
    width = -(-(flat + 1) // 128) * 128

    def step(t, acc):
        idx = lax.dynamic_slice(work_idx, (t * CHUNK,), (CHUNK,))
        rows = jnp.take(pool, idx, axis=0, mode="clip", indices_are_sorted=True)
        logits, values = evaluate(rows, *weights)
        packed = jnp.concatenate(
            [
                logits.reshape(CHUNK, flat),
                values[:, None],
                jnp.zeros((CHUNK, width - flat - 1), jnp.bfloat16),
            ],
            axis=1,
        )
        return lax.dynamic_update_slice(acc, packed, (t * CHUNK, 0))

    results = lax.fori_loop(
        0,
        (work_count + CHUNK - 1) // CHUNK,
        step,
        jnp.zeros((work_rows + margin, width), jnp.bfloat16),
    )

    back = [
        lax.ppermute(lax.dynamic_slice(results, (places[e], 0), (cap, width)), AXES, pairs[e])
        for e, cap in enumerate(caps)
    ]

    gathered = jnp.take(
        jnp.concatenate([results] + back, axis=0), lists[1, :slot_count], axis=0, mode="clip"
    )
    slot_logits = gathered[:, :flat].reshape(slot_count, FACT, MOVES)
    slot_values = gathered[:, flat]
    slot = jnp.arange(slot_count, dtype=jnp.int32)

    alive = slot < own_count
    priors = jnp.where(
        alive[:, None, None], masked_priors(slot_logits, legal, logit_scale), 0.0
    )
    leaf_values = jnp.where(alive, slot_values.astype(jnp.float32), 0.0)
    tree_total = TREE_DEV * groups
    onehot = (owners[:, None] == jnp.arange(tree_total, dtype=jnp.int32)[None, :]).astype(
        jnp.float32
    )
    partial_sums = jnp.dot(leaf_values, onehot, precision=lax.Precision.HIGHEST)
    spread = lax.all_to_all(partial_sums.reshape(groups, TREE_DEV), AXES, 0, 0, tiled=True)
    tree_value = jnp.sum(spread, axis=0)
    return (priors, leaf_values, tree_value)


def solution(mesh):
    in_specs = (
        P(AXES, None),
        P(AXES),
        P(AXES),
        P(AXES, None, None),
        P(),
        P(),
        P(),
        P(),
        P(),
        P(),
        P(),
    )
    out_specs = (P(AXES, None, None), P(AXES), P(AXES))
    return jax.shard_map(body, mesh=mesh, in_specs=in_specs, out_specs=out_specs, check_vma=False)
```

```python
import functools

import jax
import jax.numpy as jnp
from jax import lax
from jax.experimental import pallas as pl
from jax.experimental.pallas import tpu as pltpu
from jax.sharding import PartitionSpec as P

SIDE = 19
BOARD = 361
MOVES = 362
PLANES = 32
FACT = 8
TREE_DEV = 8
AXES = ("search", "net")
CHUNK = 40
PASSES = 5
CORE_CAP = 64
LINK_CAP = 32
FAR_CAP = 16


def convolve(inputs, kernel):
    return lax.conv_general_dilated(
        inputs,
        kernel,
        (1, 1),
        "SAME",
        dimension_numbers=("NHWC", "HWIO", "NHWC"),
        preferred_element_type=jnp.float32,
    )


def evaluate(batch, in_weight, mid_weight, out_weight, policy_weight, pass_weight, value_weight):
    leaves = batch.shape[0]
    board = batch.reshape(leaves, SIDE, SIDE, PLANES)
    hidden = jax.nn.relu(convolve(board, in_weight)).astype(jnp.bfloat16)
    inner = jax.nn.relu(convolve(hidden, mid_weight[0])).astype(jnp.bfloat16)
    hidden = jax.nn.relu(hidden.astype(jnp.float32) + convolve(inner, out_weight[0])).astype(
        jnp.bfloat16
    )
    cells = jnp.einsum(
        "bhwc,cf->bfhw", hidden, policy_weight, preferred_element_type=jnp.float32
    ).reshape(leaves, FACT, BOARD)
    pooled = jnp.mean(hidden, axis=(1, 2), dtype=jnp.float32)
    passing = jnp.dot(pooled, pass_weight.astype(jnp.float32), precision=lax.Precision.HIGHEST)
    logits = jnp.concatenate([cells, passing[:, :, None]], axis=2).astype(jnp.bfloat16)
    values = jnp.tanh(
        jnp.dot(pooled, value_weight.astype(jnp.float32), precision=lax.Precision.HIGHEST)
    ).astype(jnp.bfloat16)
    return (logits, values)


def masked_priors(logits, legal, logit_scale):
    scaled = logit_scale[None, :, None] * logits.astype(jnp.float32)
    allowed = jnp.concatenate(
        [legal > 0, jnp.ones(legal.shape[:2] + (1,), dtype=jnp.bool_)], axis=2
    )
    peak = jnp.max(jnp.where(allowed, scaled, -1e30), axis=2, keepdims=True)
    weights = jnp.exp(jnp.where(allowed, scaled - peak, -1e30))
    return weights / jnp.sum(weights, axis=2, keepdims=True)


def plan_kernel(masks, caps, slot_count, work_rows, counts_ref, me_ref, out_ref, idx_ref):
    counts_all = counts_ref[...]
    lanes = counts_all.shape[1]
    lane = lax.broadcasted_iota(jnp.int32, counts_all.shape, 1)

    takes_up = {m: pltpu.roll(lane, m, 1) == (lane ^ m) for m in masks}

    def swap(x, mask):
        return jnp.where(takes_up[mask], pltpu.roll(x, mask, 1), pltpu.roll(x, lanes - mask, 1))

    flows = [jnp.zeros_like(counts_all) for _ in masks]
    sent = jnp.zeros_like(counts_all)
    got = jnp.zeros_like(counts_all)
    for _ in range(PASSES):
        for e, (mask, cap) in enumerate(zip(masks, caps)):
            load = counts_all - sent + got
            own = counts_all - sent
            move = jnp.right_shift(jnp.maximum(load - swap(load, mask), 0), 1)
            cancel = jnp.minimum(move, swap(flows[e], mask))
            add = jnp.clip(move - cancel, 0, jnp.minimum(cap - flows[e], own))
            cancelled = swap(cancel, mask)
            flows[e] = flows[e] + add - cancelled
            sent = sent + add - cancelled
            got = got + swap(add, mask) - cancel
    into = [swap(f, m) for f, m in zip(flows, masks)]
    keep = counts_all - sum(flows)
    starts, places = [], []
    for e in range(len(masks)):
        starts.append(keep + sum(flows[:e]))
        places.append(keep + sum(into[:e]))
    rows = flows + into + starts + places + [keep, keep + sum(into)]
    rows = rows + [jnp.zeros_like(counts_all)] * (out_ref.shape[0] - len(rows))
    out_ref[...] = jnp.concatenate(rows, axis=0)

    me = me_ref[...]

    def mine(v):
        return jnp.sum(jnp.where(lane == me, v, 0), axis=1, keepdims=True)

    k = lax.broadcasted_iota(jnp.int32, (1, idx_ref.shape[1]), 1)
    work_idx = k
    pick = k
    work_base = slot_count
    pick_base = work_rows + max(caps)
    for e, cap in enumerate(caps):
        place, got_e = mine(places[e]), mine(into[e])
        work_idx = jnp.where((k >= place) & (k < place + got_e), work_base + k - place, work_idx)
        start, sent_e = mine(starts[e]), mine(flows[e])
        pick = jnp.where((k >= start) & (k < start + sent_e), pick_base + k - start, pick)
        work_base = work_base + cap
        pick_base = pick_base + cap
    work_idx = jnp.where(k < mine(keep + sum(into)), jnp.clip(work_idx, 0, work_base - 1), work_base - 1)
    pick = jnp.clip(pick, 0, pick_base - 1)
    idx_ref[...] = jnp.concatenate([work_idx, pick] + [k * 0] * (idx_ref.shape[0] - 2), axis=0)


def make_plan(counts_all, me, masks, caps, slot_count, work_rows):
    groups = counts_all.shape[0]
    lanes = -(-groups // 128) * 128
    padded = jnp.zeros((1, lanes), jnp.int32).at[0, :groups].set(counts_all)
    rows = -(-(4 * len(masks) + 2) // 8) * 8
    width = -(-max(work_rows, slot_count) // 128) * 128
    return pl.pallas_call(
        functools.partial(plan_kernel, masks, caps, slot_count, work_rows),
        out_shape=(
            jax.ShapeDtypeStruct((rows, lanes), jnp.int32),
            jax.ShapeDtypeStruct((8, width), jnp.int32),
        ),
    )(padded, jnp.full((1, lanes), me, jnp.int32))


def body(
    states,
    counts,
    owners,
    legal,
    in_weight,
    mid_weight,
    out_weight,
    policy_weight,
    pass_weight,
    value_weight,
    logit_scale,
):
    weights = (in_weight, mid_weight, out_weight, policy_weight, pass_weight, value_weight)
    slot_count, row = states.shape
    groups = lax.axis_size(AXES)
    net_size = lax.axis_size("net")
    me = lax.axis_index(AXES)
    own_count = counts[0]

    counts_all = lax.all_to_all(
        jnp.broadcast_to(counts, (groups, 1)), AXES, 0, 0, tiled=True
    ).reshape(groups)

    masks = (4, 2, 2 * net_size, 1, net_size)
    caps = (FAR_CAP, LINK_CAP, LINK_CAP, LINK_CAP, CORE_CAP)
    work_rows = -(-slot_count // CHUNK) * CHUNK
    plan, lists = make_plan(counts_all, me, masks, caps, slot_count, work_rows)
    mine = lax.dynamic_slice(plan, (0, me), (plan.shape[0], 1))[:, 0]
    edges = len(masks)
    send = [mine[e] for e in range(edges)]
    starts = [mine[2 * edges + e] for e in range(edges)]
    places = [mine[3 * edges + e] for e in range(edges)]
    work_count = mine[4 * edges + 1]

    recv = [mine[edges + e] for e in range(edges)]

    margin = max(caps)
    padded = jnp.concatenate([states, jnp.zeros((margin, row), states.dtype)])
    pairs = [[(d, d ^ m) for d in range(groups)] for m in masks]
    incoming = [
        lax.ppermute(lax.dynamic_slice(padded, (starts[e], 0), (cap, row)), AXES, pairs[e])
        for e, cap in enumerate(caps)
    ]

    pool = jnp.concatenate([states] + incoming, axis=0)
    work_idx = lists[0, :work_rows]
    flat = FACT * MOVES
    width = -(-(flat + 1) // 128) * 128

    def step(t, acc):
        idx = lax.dynamic_slice(work_idx, (t * CHUNK,), (CHUNK,))
        rows = jnp.take(pool, idx, axis=0, mode="clip", indices_are_sorted=True)
        logits, values = evaluate(rows, *weights)
        packed = jnp.concatenate(
            [
                logits.reshape(CHUNK, flat),
                values[:, None],
                jnp.zeros((CHUNK, width - flat - 1), jnp.bfloat16),
            ],
            axis=1,
        )
        return lax.dynamic_update_slice(acc, packed, (t * CHUNK, 0))

    results = lax.fori_loop(
        0,
        (work_count + CHUNK - 1) // CHUNK,
        step,
        jnp.zeros((work_rows + margin, width), jnp.bfloat16),
    )

    back = [
        lax.ppermute(lax.dynamic_slice(results, (places[e], 0), (cap, width)), AXES, pairs[e])
        for e, cap in enumerate(caps)
    ]

    gathered = jnp.take(
        jnp.concatenate([results] + back, axis=0), lists[1, :slot_count], axis=0, mode="clip"
    )
    slot_logits = gathered[:, :flat].reshape(slot_count, FACT, MOVES)
    slot_values = gathered[:, flat]
    slot = jnp.arange(slot_count, dtype=jnp.int32)

    alive = slot < own_count
    priors = jnp.where(
        alive[:, None, None], masked_priors(slot_logits, legal, logit_scale), 0.0
    )
    leaf_values = jnp.where(alive, slot_values.astype(jnp.float32), 0.0)
    tree_total = TREE_DEV * groups
    onehot = (owners[:, None] == jnp.arange(tree_total, dtype=jnp.int32)[None, :]).astype(
        jnp.float32
    )
    partial_sums = jnp.dot(leaf_values, onehot, precision=lax.Precision.HIGHEST)
    spread = lax.all_to_all(partial_sums.reshape(groups, TREE_DEV), AXES, 0, 0, tiled=True)
    tree_value = jnp.sum(spread, axis=0)
    return (priors, leaf_values, tree_value)


def solution(mesh):
    in_specs = (
        P(AXES, None),
        P(AXES),
        P(AXES),
        P(AXES, None, None),
        P(),
        P(),
        P(),
        P(),
        P(),
        P(),
        P(),
    )
    out_specs = (P(AXES, None, None), P(AXES), P(AXES))
    return jax.shard_map(body, mesh=mesh, in_specs=in_specs, out_specs=out_specs, check_vma=False)
```

```python
import functools

import jax
import jax.numpy as jnp
from jax import lax
from jax.experimental import pallas as pl
from jax.experimental.pallas import tpu as pltpu
from jax.sharding import PartitionSpec as P

SIDE = 19
BOARD = 361
MOVES = 362
PLANES = 32
FACT = 8
TREE_DEV = 8
AXES = ("search", "net")
CHUNK = 40
PASSES = 5
CORE_CAP = 48
LINK_CAP = 32
FAR_CAP = 16


def convolve(inputs, kernel):
    return lax.conv_general_dilated(
        inputs,
        kernel,
        (1, 1),
        "SAME",
        dimension_numbers=("NHWC", "HWIO", "NHWC"),
        preferred_element_type=jnp.float32,
    )


def evaluate(batch, in_weight, mid_weight, out_weight, policy_weight, pass_weight, value_weight):
    leaves = batch.shape[0]
    board = batch.reshape(leaves, SIDE, SIDE, PLANES)
    hidden = jax.nn.relu(convolve(board, in_weight)).astype(jnp.bfloat16)
    inner = jax.nn.relu(convolve(hidden, mid_weight[0])).astype(jnp.bfloat16)
    hidden = jax.nn.relu(hidden.astype(jnp.float32) + convolve(inner, out_weight[0])).astype(
        jnp.bfloat16
    )
    cells = jnp.einsum(
        "bhwc,cf->bfhw", hidden, policy_weight, preferred_element_type=jnp.float32
    ).reshape(leaves, FACT, BOARD)
    pooled = jnp.mean(hidden, axis=(1, 2), dtype=jnp.float32)
    passing = jnp.dot(pooled, pass_weight.astype(jnp.float32), precision=lax.Precision.HIGHEST)
    logits = jnp.concatenate([cells, passing[:, :, None]], axis=2).astype(jnp.bfloat16)
    values = jnp.tanh(
        jnp.dot(pooled, value_weight.astype(jnp.float32), precision=lax.Precision.HIGHEST)
    ).astype(jnp.bfloat16)
    return (logits, values)


def masked_priors(logits, legal, logit_scale):
    scaled = logit_scale[None, :, None] * logits.astype(jnp.float32)
    allowed = jnp.concatenate(
        [legal > 0, jnp.ones(legal.shape[:2] + (1,), dtype=jnp.bool_)], axis=2
    )
    peak = jnp.max(jnp.where(allowed, scaled, -1e30), axis=2, keepdims=True)
    weights = jnp.exp(jnp.where(allowed, scaled - peak, -1e30))
    return weights / jnp.sum(weights, axis=2, keepdims=True)


def plan_kernel(masks, caps, slot_count, work_rows, counts_ref, me_ref, out_ref, idx_ref):
    counts_all = counts_ref[...]
    lanes = counts_all.shape[1]
    lane = lax.broadcasted_iota(jnp.int32, counts_all.shape, 1)

    takes_up = {m: pltpu.roll(lane, m, 1) == (lane ^ m) for m in masks}

    def swap(x, mask):
        return jnp.where(takes_up[mask], pltpu.roll(x, mask, 1), pltpu.roll(x, lanes - mask, 1))

    flows = [jnp.zeros_like(counts_all) for _ in masks]
    sent = jnp.zeros_like(counts_all)
    got = jnp.zeros_like(counts_all)
    for _ in range(PASSES):
        for e, (mask, cap) in enumerate(zip(masks, caps)):
            load = counts_all - sent + got
            own = counts_all - sent
            move = jnp.right_shift(jnp.maximum(load - swap(load, mask), 0), 1)
            cancel = jnp.minimum(move, swap(flows[e], mask))
            add = jnp.clip(move - cancel, 0, jnp.minimum(cap - flows[e], own))
            cancelled = swap(cancel, mask)
            flows[e] = flows[e] + add - cancelled
            sent = sent + add - cancelled
            got = got + swap(add, mask) - cancel
    into = [swap(f, m) for f, m in zip(flows, masks)]
    keep = counts_all - sum(flows)
    starts, places = [], []
    for e in range(len(masks)):
        starts.append(keep + sum(flows[:e]))
        places.append(keep + sum(into[:e]))
    rows = flows + into + starts + places + [keep, keep + sum(into)]
    rows = rows + [jnp.zeros_like(counts_all)] * (out_ref.shape[0] - len(rows))
    out_ref[...] = jnp.concatenate(rows, axis=0)

    me = me_ref[...]

    def mine(v):
        return jnp.sum(jnp.where(lane == me, v, 0), axis=1, keepdims=True)

    k = lax.broadcasted_iota(jnp.int32, (1, idx_ref.shape[1]), 1)
    work_idx = k
    pick = k
    work_base = slot_count
    pick_base = work_rows + max(caps)
    for e, cap in enumerate(caps):
        place, got_e = mine(places[e]), mine(into[e])
        work_idx = jnp.where((k >= place) & (k < place + got_e), work_base + k - place, work_idx)
        start, sent_e = mine(starts[e]), mine(flows[e])
        pick = jnp.where((k >= start) & (k < start + sent_e), pick_base + k - start, pick)
        work_base = work_base + cap
        pick_base = pick_base + cap
    work_idx = jnp.where(k < mine(keep + sum(into)), jnp.clip(work_idx, 0, work_base - 1), work_base - 1)
    pick = jnp.clip(pick, 0, pick_base - 1)
    idx_ref[...] = jnp.concatenate([work_idx, pick] + [k * 0] * (idx_ref.shape[0] - 2), axis=0)


def make_plan(counts_all, me, masks, caps, slot_count, work_rows):
    groups = counts_all.shape[0]
    lanes = -(-groups // 128) * 128
    padded = jnp.zeros((1, lanes), jnp.int32).at[0, :groups].set(counts_all)
    rows = -(-(4 * len(masks) + 2) // 8) * 8
    width = -(-max(work_rows, slot_count) // 128) * 128
    return pl.pallas_call(
        functools.partial(plan_kernel, masks, caps, slot_count, work_rows),
        out_shape=(
            jax.ShapeDtypeStruct((rows, lanes), jnp.int32),
            jax.ShapeDtypeStruct((8, width), jnp.int32),
        ),
    )(padded, jnp.full((1, lanes), me, jnp.int32))


def body(
    states,
    counts,
    owners,
    legal,
    in_weight,
    mid_weight,
    out_weight,
    policy_weight,
    pass_weight,
    value_weight,
    logit_scale,
):
    weights = (in_weight, mid_weight, out_weight, policy_weight, pass_weight, value_weight)
    slot_count, row = states.shape
    groups = lax.axis_size(AXES)
    net_size = lax.axis_size("net")
    me = lax.axis_index(AXES)
    own_count = counts[0]

    counts_all = lax.all_to_all(
        jnp.broadcast_to(counts, (groups, 1)), AXES, 0, 0, tiled=True
    ).reshape(groups)

    masks = (4, 2, 2 * net_size, 1, net_size)
    caps = (FAR_CAP, LINK_CAP, LINK_CAP, LINK_CAP, CORE_CAP)
    work_rows = -(-slot_count // CHUNK) * CHUNK
    plan, lists = make_plan(counts_all, me, masks, caps, slot_count, work_rows)
    mine = lax.dynamic_slice(plan, (0, me), (plan.shape[0], 1))[:, 0]
    edges = len(masks)
    send = [mine[e] for e in range(edges)]
    starts = [mine[2 * edges + e] for e in range(edges)]
    places = [mine[3 * edges + e] for e in range(edges)]
    work_count = mine[4 * edges + 1]

    recv = [mine[edges + e] for e in range(edges)]

    margin = max(caps)
    padded = jnp.concatenate([states, jnp.zeros((margin, row), states.dtype)])
    pairs = [[(d, d ^ m) for d in range(groups)] for m in masks]
    incoming = [
        lax.ppermute(lax.dynamic_slice(padded, (starts[e], 0), (cap, row)), AXES, pairs[e])
        for e, cap in enumerate(caps)
    ]

    pool = jnp.concatenate([states] + incoming, axis=0)
    work_idx = lists[0, :work_rows]
    flat = FACT * MOVES
    width = -(-(flat + 1) // 128) * 128

    def step(t, acc):
        idx = lax.dynamic_slice(work_idx, (t * CHUNK,), (CHUNK,))
        rows = jnp.take(pool, idx, axis=0, mode="clip", indices_are_sorted=True)
        logits, values = evaluate(rows, *weights)
        packed = jnp.concatenate(
            [
                logits.reshape(CHUNK, flat),
                values[:, None],
                jnp.zeros((CHUNK, width - flat - 1), jnp.bfloat16),
            ],
            axis=1,
        )
        return lax.dynamic_update_slice(acc, packed, (t * CHUNK, 0))

    results = lax.fori_loop(
        0,
        (work_count + CHUNK - 1) // CHUNK,
        step,
        jnp.zeros((work_rows + margin, width), jnp.bfloat16),
    )

    back = [
        lax.ppermute(lax.dynamic_slice(results, (places[e], 0), (cap, width)), AXES, pairs[e])
        for e, cap in enumerate(caps)
    ]

    gathered = jnp.take(
        jnp.concatenate([results] + back, axis=0), lists[1, :slot_count], axis=0, mode="clip"
    )
    slot_logits = gathered[:, :flat].reshape(slot_count, FACT, MOVES)
    slot_values = gathered[:, flat]
    slot = jnp.arange(slot_count, dtype=jnp.int32)

    alive = slot < own_count
    priors = jnp.where(
        alive[:, None, None], masked_priors(slot_logits, legal, logit_scale), 0.0
    )
    leaf_values = jnp.where(alive, slot_values.astype(jnp.float32), 0.0)
    tree_total = TREE_DEV * groups
    onehot = (owners[:, None] == jnp.arange(tree_total, dtype=jnp.int32)[None, :]).astype(
        jnp.float32
    )
    partial_sums = jnp.dot(leaf_values, onehot, precision=lax.Precision.HIGHEST)
    spread = lax.all_to_all(partial_sums.reshape(groups, TREE_DEV), AXES, 0, 0, tiled=True)
    tree_value = jnp.sum(spread, axis=0)
    return (priors, leaf_values, tree_value)


def solution(mesh):
    in_specs = (
        P(AXES, None),
        P(AXES),
        P(AXES),
        P(AXES, None, None),
        P(),
        P(),
        P(),
        P(),
        P(),
        P(),
        P(),
    )
    out_specs = (P(AXES, None, None), P(AXES), P(AXES))
    return jax.shard_map(body, mesh=mesh, in_specs=in_specs, out_specs=out_specs, check_vma=False)
```
